1024 devices in a mesh: rad: 8 (over z_lo), azi: 128 (over x, z_hi, y, core).
Axes of the slice: x: 4, y: 8, z: 16 (z_hi: 2, z_lo: 8; z = z_hi * 8 + z_lo), core: 2. Of those that a mesh axis runs over, the one named last changes fastest.
Arguments:
- fields: float32 [5, 1, 8192, 1024], P(None, None, 'azi', 'rad'), may hold values from -2 to 2, as said below
- shifts: int32 [3, 1024], P(None, 'rad'), may hold values from 0 to 192, as said below
Outputs:
- advanced: float32 [5, 1, 8192, 1024], P(None, None, 'azi', 'rad')
The draws below stay inside these ranges and needn't reach their ends.
Inputs may be any that keep to these rules, and one draw needn't show every extreme that they name: `fields`: every field component lies within -2 to 2; temperature within 0.5 to 1.5. `shifts`: each step has a row with shift 192 and a row with shift 0.
All inputs are finite; a program needn't handle non-finite values.
Results may differ from the reference program's by a relative error of at most 0.00002.
Values sent between devices are 32-bit elements; how exact they have to be, the bound alone decides.
No kernel may reach another device: no remote copies, remote signals or barrier semaphores. Data moves between devices by JAX's collectives and lax.ppermute only.
A program may use at most 32 MiB of HBM per device.

```python
import jax
import jax.numpy as jnp

POL = 1
STEPS = 3
SMAX = 192
NR = 1024
NPHI = 8192


def draw_fields(key, part):
    keys = jax.random.split(key, 6)
    shape = (POL, NPHI, NR)
    log_rho = jnp.clip(0.5 * jax.random.normal(keys[0], shape, jnp.float32), -2.0, 2.0)
    vels = [jax.random.uniform(keys[i], shape, jnp.float32, -1.0, 1.0) for i in (1, 2, 3)]
    temper = jax.random.uniform(keys[4], shape, jnp.float32, 0.5, 1.5)
    return jnp.stack([log_rho, vels[0], vels[1], vels[2], temper]).astype(jnp.float32)


def draw_shifts(key, part):
    values = jax.random.randint(key, (STEPS, NR), 0, SMAX + 1, dtype=jnp.int32)
    values = values.at[:, 0].set(SMAX)
    values = values.at[:, 1].set(0)
    return values.astype(jnp.int32)


def setup_inputs(seed: int = 0) -> dict:
    streams_of = jax.random.split(jax.random.key(seed), 3)
    fields = draw_fields(jax.random.fold_in(streams_of[2], 71), 0)
    shifts = draw_shifts(jax.random.fold_in(streams_of[2], 71), 0)
    return dict(fields=fields, shifts=shifts)


courant = 0.2
viscous = 0.1


def update(padded, inverse):
    centre = padded[:, :, 1:-1, 1:-1]
    inner = padded[:, :, 1:-1, :-2]
    outer = padded[:, :, 1:-1, 2:]
    behind = padded[:, :, :-2, 1:-1]
    ahead = padded[:, :, 2:, 1:-1]
    polar_pad = jnp.concatenate([centre[:, :1], centre, centre[:, -1:]], axis=1)
    polar_sum = polar_pad[:, 2:] + polar_pad[:, :-2]
    radial_vel = centre[1]
    azim_vel = centre[2]
    advect = courant * (jnp.maximum(radial_vel, 0.0) * (centre - inner) + jnp.minimum(radial_vel, 0.0) * (outer - centre)
                        + inverse * (jnp.maximum(azim_vel, 0.0) * (centre - behind) + jnp.minimum(azim_vel, 0.0) * (ahead - centre)))
    laplace = (outer + inner - 2.0 * centre) + inverse * inverse * (ahead + behind - 2.0 * centre) + (polar_sum - 2.0 * centre)
    radial_diff = (outer - inner) * 0.5
    azim_diff = (ahead - behind) * 0.5
    diverge = radial_diff[1] + inverse * azim_diff[2]
    log_rho = centre[0]
    temper = centre[4]
    new_log = log_rho - advect[0] - courant * diverge
    new_radial = radial_vel - advect[1] - courant * (temper * radial_diff[0] + radial_diff[4]) + 0.5 * courant * inverse * azim_vel * azim_vel + viscous * laplace[1]
    new_azim = azim_vel - advect[2] - courant * inverse * (temper * azim_diff[0] + azim_diff[4]) - 0.5 * courant * inverse * radial_vel * azim_vel + viscous * laplace[2]
    new_polar = centre[3] - advect[3] + viscous * laplace[3]
    new_temper = temper - advect[4] - courant * 0.4 * temper * diverge + viscous * laplace[4]
    return jnp.stack([new_log, new_radial, new_azim, new_polar, new_temper])


def reference(fields, shifts):
    radius = 1.0 + (jnp.arange(NR).astype(jnp.float32) + 0.5) / jnp.float32(NR)
    inverse = 1.0 / radius
    cells = jnp.arange(NPHI, dtype=jnp.int32)
    for step in range(STEPS):
        radial_pad = jnp.pad(fields, ((0, 0), (0, 0), (0, 0), (1, 1)))
        padded = jnp.concatenate([radial_pad[:, :, -1:], radial_pad, radial_pad[:, :, :1]], axis=2)
        fields = update(padded, inverse)
        source = jnp.mod(cells[:, None] - shifts[step][None, :], NPHI).astype(jnp.int32)
        source = jnp.broadcast_to(source[None, None], fields.shape)
        fields = jnp.take_along_axis(fields, source, axis=2)
    return fields
```

```python
import jax
import jax.numpy as jnp
from jax import lax
from jax.sharding import PartitionSpec as P

STEPS = 3
SMAX = 192


courant = 0.2
viscous = 0.1


def passed_along(value, axis, steps, wrap=True):
    count = lax.axis_size(axis)
    if wrap:
        pairs = [(source, (source + steps) % count) for source in range(count)]
    else:
        pairs = [
            (source, source + steps)
            for source in range(count)
            if 0 <= source + steps < count
        ]
    return lax.ppermute(value, axis, pairs)


def update(padded, inverse):
    centre = padded[:, :, 1:-1, 1:-1]
    inner = padded[:, :, 1:-1, :-2]
    outer = padded[:, :, 1:-1, 2:]
    behind = padded[:, :, :-2, 1:-1]
    ahead = padded[:, :, 2:, 1:-1]
    polar_pad = jnp.concatenate([centre[:, :1], centre, centre[:, -1:]], axis=1)
    polar_sum = polar_pad[:, 2:] + polar_pad[:, :-2]
    radial_vel = centre[1]
    azim_vel = centre[2]
    advect = courant * (
        jnp.maximum(radial_vel, 0.0) * (centre - inner)
        + jnp.minimum(radial_vel, 0.0) * (outer - centre)
        + inverse
        * (
            jnp.maximum(azim_vel, 0.0) * (centre - behind)
            + jnp.minimum(azim_vel, 0.0) * (ahead - centre)
        )
    )
    laplace = (
        outer
        + inner
        - 2.0 * centre
        + inverse * inverse * (ahead + behind - 2.0 * centre)
        + (polar_sum - 2.0 * centre)
    )
    radial_diff = (outer - inner) * 0.5
    azim_diff = (ahead - behind) * 0.5
    diverge = radial_diff[1] + inverse * azim_diff[2]
    log_rho = centre[0]
    temper = centre[4]
    new_log = log_rho - advect[0] - courant * diverge
    new_radial = (
        radial_vel
        - advect[1]
        - courant * (temper * radial_diff[0] + radial_diff[4])
        + 0.5 * courant * inverse * azim_vel * azim_vel
        + viscous * laplace[1]
    )
    new_azim = (
        azim_vel
        - advect[2]
        - courant * inverse * (temper * azim_diff[0] + azim_diff[4])
        - 0.5 * courant * inverse * radial_vel * azim_vel
        + viscous * laplace[2]
    )
    new_polar = centre[3] - advect[3] + viscous * laplace[3]
    new_temper = temper - advect[4] - courant * 0.4 * temper * diverge + viscous * laplace[4]
    return jnp.stack([new_log, new_radial, new_azim, new_polar, new_temper])


def halo_exchange(fields, shifts, width):
    cells = fields.shape[2]
    last = fields[:, :, cells - width :]
    first = fields[:, :, :width]
    before = passed_along(last, "azi", 1)
    after = passed_along(first, "azi", -1)
    wide = jnp.concatenate([before, fields, after], axis=2)

    rows = wide.shape[3]
    shape = wide.shape[:3] + (width,)
    count = shape[0] * shape[1] * shape[2] * shape[3]

    def pack(lo, hi):
        part = wide[:, :, :, lo:hi].reshape(-1)
        rates = shifts[:, lo:hi].astype(jnp.float32).reshape(-1)
        return jnp.concatenate([part, rates])

    def unpack(flat):
        part = flat[:count].reshape(shape)
        rates = flat[count:].reshape(shifts.shape[0], width)
        return part, rates.astype(jnp.int32)

    inner, inner_shift = unpack(passed_along(pack(rows - width, rows), "rad", 1, False))
    outer, outer_shift = unpack(passed_along(pack(0, width), "rad", -1, False))
    wide = jnp.concatenate([inner, wide, outer], axis=3)
    wide_shifts = jnp.concatenate([inner_shift, shifts, outer_shift], axis=1)
    return wide, wide_shifts


def rotate_window(window, offsets, out_len):
    take = SMAX - offsets
    nbits = SMAX.bit_length()
    spare = (1 << nbits) - 1 + out_len - window.shape[2]
    if spare > 0:
        pad = jnp.zeros(window.shape[:2] + (spare,) + window.shape[3:], window.dtype)
        window = jnp.concatenate([window, pad], axis=2)
    for bit in range(nbits):
        amount = 1 << bit
        length = window.shape[2] - amount
        chosen = take // amount % 2 == 1
        window = jnp.where(
            chosen[None, None, None, :], window[:, :, amount:], window[:, :, :length]
        )
    return window[:, :, :out_len]


def local(fields, shifts):
    cells = fields.shape[2]
    rows = fields.shape[3]
    total_rows = rows * lax.axis_size("rad")
    width = STEPS
    wide, wide_shifts = halo_exchange(fields, shifts, width)
    start_row = lax.axis_index("rad") * rows
    blocks = (SMAX + cells - 1) // cells
    for step in range(STEPS):
        w = width - step
        row_index = start_row - w + jnp.arange(rows + 2 * w, dtype=jnp.int32)
        inside = (row_index >= 0) & (row_index < total_rows)
        wide = jnp.where(inside[None, None, None, :], wide, 0.0)
        inner_rows = row_index[1:-1]
        radius = 1.0 + (inner_rows.astype(jnp.float32) + 0.5) / jnp.float32(total_rows)
        inverse = 1.0 / radius
        updated = update(wide, inverse)
        a = w - 1
        head = updated[:, :, :cells]
        pieces = [passed_along(head, "azi", k) for k in range(blocks, 0, -1)]
        window = jnp.concatenate(pieces + [updated], axis=2)
        window = window[:, :, blocks * cells - SMAX :]
        wide_shifts = wide_shifts[:, 1:-1]
        wide = rotate_window(window, wide_shifts[step], cells + 2 * a)
    return wide


def solution(mesh):
    placed = (P(None, None, "azi", "rad"), P(None, "rad"))
    return jax.shard_map(
        local, mesh=mesh, in_specs=placed, out_specs=P(None, None, "azi", "rad"), check_vma=False
    )
```

```python
import jax
import jax.numpy as jnp
from jax import lax
from jax.sharding import PartitionSpec as P

STEPS = 3
SMAX = 192
PLANE = 16


courant = 0.2
viscous = 0.1


def passed_along(value, axis, steps, wrap=True):
    count = lax.axis_size(axis)
    if wrap:
        pairs = [(source, (source + steps) % count) for source in range(count)]
    else:
        pairs = [
            (source, source + steps)
            for source in range(count)
            if 0 <= source + steps < count
        ]
    return lax.ppermute(value, axis, pairs)


def update(padded, inverse):
    centre = padded[:, :, 1:-1, 1:-1]
    inner = padded[:, :, 1:-1, :-2]
    outer = padded[:, :, 1:-1, 2:]
    behind = padded[:, :, :-2, 1:-1]
    ahead = padded[:, :, 2:, 1:-1]
    polar_pad = jnp.concatenate([centre[:, :1], centre, centre[:, -1:]], axis=1)
    polar_sum = polar_pad[:, 2:] + polar_pad[:, :-2]
    radial_vel = centre[1]
    azim_vel = centre[2]
    advect = courant * (
        jnp.maximum(radial_vel, 0.0) * (centre - inner)
        + jnp.minimum(radial_vel, 0.0) * (outer - centre)
        + inverse
        * (
            jnp.maximum(azim_vel, 0.0) * (centre - behind)
            + jnp.minimum(azim_vel, 0.0) * (ahead - centre)
        )
    )
    laplace = (
        outer
        + inner
        - 2.0 * centre
        + inverse * inverse * (ahead + behind - 2.0 * centre)
        + (polar_sum - 2.0 * centre)
    )
    radial_diff = (outer - inner) * 0.5
    azim_diff = (ahead - behind) * 0.5
    diverge = radial_diff[1] + inverse * azim_diff[2]
    log_rho = centre[0]
    temper = centre[4]
    new_log = log_rho - advect[0] - courant * diverge
    new_radial = (
        radial_vel
        - advect[1]
        - courant * (temper * radial_diff[0] + radial_diff[4])
        + 0.5 * courant * inverse * azim_vel * azim_vel
        + viscous * laplace[1]
    )
    new_azim = (
        azim_vel
        - advect[2]
        - courant * inverse * (temper * azim_diff[0] + azim_diff[4])
        - 0.5 * courant * inverse * radial_vel * azim_vel
        + viscous * laplace[2]
    )
    new_polar = centre[3] - advect[3] + viscous * laplace[3]
    new_temper = temper - advect[4] - courant * 0.4 * temper * diverge + viscous * laplace[4]
    return jnp.stack([new_log, new_radial, new_azim, new_polar, new_temper])


def halo_exchange(fields, shifts, width):
    cells = fields.shape[2]
    last = fields[:, :, cells - width :]
    first = fields[:, :, :width]
    before = passed_along(last, "azi", 1)
    after = passed_along(first, "azi", -1)
    wide = jnp.concatenate([before, fields, after], axis=2)

    rows = wide.shape[3]
    shape = wide.shape[:3] + (width,)
    count = shape[0] * shape[1] * shape[2] * shape[3]

    def pack(lo, hi):
        part = wide[:, :, :, lo:hi].reshape(-1)
        rates = shifts[:, lo:hi].astype(jnp.float32).reshape(-1)
        return jnp.concatenate([part, rates])

    def unpack(flat):
        part = flat[:count].reshape(shape)
        rates = flat[count:].reshape(shifts.shape[0], width)
        return part, rates.astype(jnp.int32)

    inner, inner_shift = unpack(passed_along(pack(rows - width, rows), "rad", 1, False))
    outer, outer_shift = unpack(passed_along(pack(0, width), "rad", -1, False))
    wide = jnp.concatenate([inner, wide, outer], axis=3)
    wide_shifts = jnp.concatenate([inner_shift, shifts, outer_shift], axis=1)
    return wide, wide_shifts


def rotate_window(window, offsets, out_len):
    take = SMAX - offsets
    nbits = SMAX.bit_length()
    spare = (1 << nbits) - 1 + out_len - window.shape[2]
    if spare > 0:
        pad = jnp.zeros(window.shape[:2] + (spare,) + window.shape[3:], window.dtype)
        window = jnp.concatenate([window, pad], axis=2)
    for bit in range(nbits):
        amount = 1 << bit
        length = window.shape[2] - amount
        chosen = take // amount % 2 == 1
        window = jnp.where(
            chosen[None, None, None, :], window[:, :, amount:], window[:, :, :length]
        )
    return window[:, :, :out_len]


def crossing_relays(groups, count, plane, blocks):
    half = plane // 2
    first, second = [], [[] for _ in range(blocks)]
    for g in range(groups):
        for block in range(count // plane):
            base = block * plane
            after = (base + plane) % count
            relay = {}
            for j in range(1, blocks + 1):
                lane = (3 * g + j - 1) % half
                relay[j] = base + 2 * lane + (j - 1) // 2
                first.append((g * count + base + plane - j, g * count + relay[j]))
            for k in range(1, blocks + 1):
                for i in range(k):
                    second[k - 1].append((g * count + relay[k - i], g * count + after + i))
    return first, second


def rotation_pieces(head, plane, blocks):
    count = lax.axis_size("azi")
    groups = lax.axis_size("rad")
    if count % plane or count <= plane or plane < 2 * blocks:
        return [passed_along(head, "azi", k) for k in range(1, blocks + 1)]
    near = []
    for k in range(1, blocks + 1):
        pairs = [
            (a, (a + k) % count)
            for a in range(count)
            if a // plane == ((a + k) % count) // plane
        ]
        near.append(lax.ppermute(head, "azi", pairs))
    first, second = crossing_relays(groups, count, plane, blocks)
    relayed = lax.ppermute(head, ("rad", "azi"), first)
    position = lax.axis_index("azi") % plane
    pieces = []
    for k in range(1, blocks + 1):
        far = lax.ppermute(relayed, ("rad", "azi"), second[k - 1])
        pieces.append(jnp.where(position < k, far, near[k - 1]))
    return pieces


def local(fields, shifts):
    cells = fields.shape[2]
    rows = fields.shape[3]
    total_rows = rows * lax.axis_size("rad")
    width = STEPS
    wide, wide_shifts = halo_exchange(fields, shifts, width)
    start_row = lax.axis_index("rad") * rows
    blocks = (SMAX + cells - 1) // cells
    for step in range(STEPS):
        w = width - step
        row_index = start_row - w + jnp.arange(rows + 2 * w, dtype=jnp.int32)
        inside = (row_index >= 0) & (row_index < total_rows)
        wide = jnp.where(inside[None, None, None, :], wide, 0.0)
        inner_rows = row_index[1:-1]
        radius = 1.0 + (inner_rows.astype(jnp.float32) + 0.5) / jnp.float32(total_rows)
        inverse = 1.0 / radius
        updated = update(wide, inverse)
        a = w - 1
        head = updated[:, :, :cells]
        pieces = rotation_pieces(head, PLANE, blocks)
        window = jnp.concatenate(pieces[::-1] + [updated], axis=2)
        window = window[:, :, blocks * cells - SMAX :]
        wide_shifts = wide_shifts[:, 1:-1]
        wide = rotate_window(window, wide_shifts[step], cells + 2 * a)
    return wide


def solution(mesh):
    placed = (P(None, None, "azi", "rad"), P(None, "rad"))
    return jax.shard_map(
        local, mesh=mesh, in_specs=placed, out_specs=P(None, None, "azi", "rad"), check_vma=False
    )
```

```python
import jax
import jax.numpy as jnp
from jax import lax
from jax.sharding import PartitionSpec as P

STEPS = 3
SMAX = 192
PLANE = 16


courant = 0.2
viscous = 0.1


def passed_along(value, axis, steps, wrap=True):
    count = lax.axis_size(axis)
    if wrap:
        pairs = [(source, (source + steps) % count) for source in range(count)]
    else:
        pairs = [
            (source, source + steps)
            for source in range(count)
            if 0 <= source + steps < count
        ]
    return lax.ppermute(value, axis, pairs)


def update(padded, inverse):
    centre = padded[:, :, 1:-1, 1:-1]
    inner = padded[:, :, 1:-1, :-2]
    outer = padded[:, :, 1:-1, 2:]
    behind = padded[:, :, :-2, 1:-1]
    ahead = padded[:, :, 2:, 1:-1]
    polar_pad = jnp.concatenate([centre[:, :1], centre, centre[:, -1:]], axis=1)
    polar_sum = polar_pad[:, 2:] + polar_pad[:, :-2]
    radial_vel = centre[1]
    azim_vel = centre[2]
    advect = courant * (
        jnp.maximum(radial_vel, 0.0) * (centre - inner)
        + jnp.minimum(radial_vel, 0.0) * (outer - centre)
        + inverse
        * (
            jnp.maximum(azim_vel, 0.0) * (centre - behind)
            + jnp.minimum(azim_vel, 0.0) * (ahead - centre)
        )
    )
    laplace = (
        outer
        + inner
        - 2.0 * centre
        + inverse * inverse * (ahead + behind - 2.0 * centre)
        + (polar_sum - 2.0 * centre)
    )
    radial_diff = (outer - inner) * 0.5
    azim_diff = (ahead - behind) * 0.5
    diverge = radial_diff[1] + inverse * azim_diff[2]
    log_rho = centre[0]
    temper = centre[4]
    new_log = log_rho - advect[0] - courant * diverge
    new_radial = (
        radial_vel
        - advect[1]
        - courant * (temper * radial_diff[0] + radial_diff[4])
        + 0.5 * courant * inverse * azim_vel * azim_vel
        + viscous * laplace[1]
    )
    new_azim = (
        azim_vel
        - advect[2]
        - courant * inverse * (temper * azim_diff[0] + azim_diff[4])
        - 0.5 * courant * inverse * radial_vel * azim_vel
        + viscous * laplace[2]
    )
    new_polar = centre[3] - advect[3] + viscous * laplace[3]
    new_temper = temper - advect[4] - courant * 0.4 * temper * diverge + viscous * laplace[4]
    return jnp.stack([new_log, new_radial, new_azim, new_polar, new_temper])


def halo_exchange(fields, shifts, width):
    cells = fields.shape[2]
    last = fields[:, :, cells - width :]
    first = fields[:, :, :width]
    before = passed_along(last, "azi", 1)
    after = passed_along(first, "azi", -1)
    wide = jnp.concatenate([before, fields, after], axis=2)

    rows = wide.shape[3]
    shape = wide.shape[:3] + (width,)
    count = shape[0] * shape[1] * shape[2] * shape[3]

    def pack(lo, hi):
        part = wide[:, :, :, lo:hi].reshape(-1)
        rates = shifts[:, lo:hi].astype(jnp.float32).reshape(-1)
        return jnp.concatenate([part, rates])

    def unpack(flat):
        part = flat[:count].reshape(shape)
        rates = flat[count:].reshape(shifts.shape[0], width)
        return part, rates.astype(jnp.int32)

    inner, inner_shift = unpack(passed_along(pack(rows - width, rows), "rad", 1, False))
    outer, outer_shift = unpack(passed_along(pack(0, width), "rad", -1, False))
    wide = jnp.concatenate([inner, wide, outer], axis=3)
    wide_shifts = jnp.concatenate([inner_shift, shifts, outer_shift], axis=1)
    return wide, wide_shifts


def rotate_window(window, offsets, out_len):
    take = SMAX - offsets
    nbits = SMAX.bit_length()
    spare = (1 << nbits) - 1 + out_len - window.shape[2]
    if spare > 0:
        pad = jnp.zeros(window.shape[:2] + (spare,) + window.shape[3:], window.dtype)
        window = jnp.concatenate([window, pad], axis=2)
    for bit in range(nbits):
        amount = 1 << bit
        length = window.shape[2] - amount
        chosen = take // amount % 2 == 1
        window = jnp.where(
            chosen[None, None, None, :], window[:, :, amount:], window[:, :, :length]
        )
    return window[:, :, :out_len]


def relay_seat(lane, source, plane, blocks):
    if source // 2 == lane:
        return source
    if 2 * lane + 1 < plane - blocks and 2 * lane < blocks:
        return 2 * lane + 1
    return 2 * lane


def crossing_relays(groups, count, plane, blocks):
    half = plane // 2
    first, second = [], [[] for _ in range(blocks)]
    for g in range(groups):
        for block in range(count // plane):
            base = block * plane
            after = (base + plane) % count
            relay = {}
            for j in range(1, blocks + 1):
                lane = (3 * g + j - 1) % half
                relay[j] = base + relay_seat(lane, plane - j, plane, blocks)
                first.append((g * count + base + plane - j, g * count + relay[j]))
            for k in range(1, blocks + 1):
                for i in range(k):
                    second[k - 1].append((g * count + relay[k - i], g * count + after + i))
    return first, second


def rotation_pieces(head, plane, blocks):
    count = lax.axis_size("azi")
    groups = lax.axis_size("rad")
    if count % plane or count <= plane or plane < 2 * blocks:
        return [passed_along(head, "azi", k) for k in range(1, blocks + 1)]
    near = []
    for k in range(1, blocks + 1):
        pairs = [
            (a, (a + k) % count)
            for a in range(count)
            if a // plane == ((a + k) % count) // plane
        ]
        near.append(lax.ppermute(head, "azi", pairs))
    first, second = crossing_relays(groups, count, plane, blocks)
    relayed = lax.ppermute(head, ("rad", "azi"), first)
    near_and_relayed = lax.optimization_barrier((near, relayed))
    near, relayed = near_and_relayed
    position = lax.axis_index("azi") % plane
    pieces = []
    for k in range(1, blocks + 1):
        far = lax.ppermute(relayed, ("rad", "azi"), second[k - 1])
        pieces.append(jnp.where(position < k, far, near[k - 1]))
    return pieces


def local(fields, shifts):
    cells = fields.shape[2]
    rows = fields.shape[3]
    total_rows = rows * lax.axis_size("rad")
    width = STEPS
    wide, wide_shifts = halo_exchange(fields, shifts, width)
    start_row = lax.axis_index("rad") * rows
    blocks = (SMAX + cells - 1) // cells
    for step in range(STEPS):
        w = width - step
        row_index = start_row - w + jnp.arange(rows + 2 * w, dtype=jnp.int32)
        inside = (row_index >= 0) & (row_index < total_rows)
        wide = jnp.where(inside[None, None, None, :], wide, 0.0)
        inner_rows = row_index[1:-1]
        radius = 1.0 + (inner_rows.astype(jnp.float32) + 0.5) / jnp.float32(total_rows)
        inverse = 1.0 / radius
        updated = update(wide, inverse)
        a = w - 1
        head = updated[:, :, :cells]
        pieces = rotation_pieces(head, PLANE, blocks)
        window = jnp.concatenate(pieces[::-1] + [updated], axis=2)
        window = window[:, :, blocks * cells - SMAX :]
        wide_shifts = wide_shifts[:, 1:-1]
        wide = rotate_window(window, wide_shifts[step], cells + 2 * a)
    return wide


def solution(mesh):
    placed = (P(None, None, "azi", "rad"), P(None, "rad"))
    return jax.shard_map(
        local, mesh=mesh, in_specs=placed, out_specs=P(None, None, "azi", "rad"), check_vma=False
    )
```

```python
import jax
import jax.numpy as jnp
from jax import lax
from jax.sharding import PartitionSpec as P

STEPS = 3
SMAX = 192
PLANE = 16


courant = 0.2
viscous = 0.1


def passed_along(value, axis, steps, wrap=True):
    count = lax.axis_size(axis)
    if wrap:
        pairs = [(source, (source + steps) % count) for source in range(count)]
    else:
        pairs = [
            (source, source + steps)
            for source in range(count)
            if 0 <= source + steps < count
        ]
    return lax.ppermute(value, axis, pairs)


def update(padded, inverse):
    centre = padded[:, :, 1:-1, 1:-1]
    inner = padded[:, :, 1:-1, :-2]
    outer = padded[:, :, 1:-1, 2:]
    behind = padded[:, :, :-2, 1:-1]
    ahead = padded[:, :, 2:, 1:-1]
    polar_pad = jnp.concatenate([centre[:, :1], centre, centre[:, -1:]], axis=1)
    polar_sum = polar_pad[:, 2:] + polar_pad[:, :-2]
    radial_vel = centre[1]
    azim_vel = centre[2]
    advect = courant * (
        jnp.maximum(radial_vel, 0.0) * (centre - inner)
        + jnp.minimum(radial_vel, 0.0) * (outer - centre)
        + inverse
        * (
            jnp.maximum(azim_vel, 0.0) * (centre - behind)
            + jnp.minimum(azim_vel, 0.0) * (ahead - centre)
        )
    )
    laplace = (
        outer
        + inner
        - 2.0 * centre
        + inverse * inverse * (ahead + behind - 2.0 * centre)
        + (polar_sum - 2.0 * centre)
    )
    radial_diff = (outer - inner) * 0.5
    azim_diff = (ahead - behind) * 0.5
    diverge = radial_diff[1] + inverse * azim_diff[2]
    log_rho = centre[0]
    temper = centre[4]
    new_log = log_rho - advect[0] - courant * diverge
    new_radial = (
        radial_vel
        - advect[1]
        - courant * (temper * radial_diff[0] + radial_diff[4])
        + 0.5 * courant * inverse * azim_vel * azim_vel
        + viscous * laplace[1]
    )
    new_azim = (
        azim_vel
        - advect[2]
        - courant * inverse * (temper * azim_diff[0] + azim_diff[4])
        - 0.5 * courant * inverse * radial_vel * azim_vel
        + viscous * laplace[2]
    )
    new_polar = centre[3] - advect[3] + viscous * laplace[3]
    new_temper = temper - advect[4] - courant * 0.4 * temper * diverge + viscous * laplace[4]
    return jnp.stack([new_log, new_radial, new_azim, new_polar, new_temper])


def halo_exchange(fields, shifts, width):
    cells = fields.shape[2]
    last = fields[:, :, cells - width :]
    first = fields[:, :, :width]
    before = passed_along(last, "azi", 1)
    after = passed_along(first, "azi", -1)
    wide = jnp.concatenate([before, fields, after], axis=2)

    rows = wide.shape[3]
    shape = wide.shape[:3] + (width,)
    count = shape[0] * shape[1] * shape[2] * shape[3]

    def pack(lo, hi):
        part = wide[:, :, :, lo:hi].reshape(-1)
        rates = shifts[:, lo:hi].astype(jnp.float32).reshape(-1)
        return jnp.concatenate([part, rates])

    def unpack(flat):
        part = flat[:count].reshape(shape)
        rates = flat[count:].reshape(shifts.shape[0], width)
        return part, rates.astype(jnp.int32)

    inner, inner_shift = unpack(passed_along(pack(rows - width, rows), "rad", 1, False))
    outer, outer_shift = unpack(passed_along(pack(0, width), "rad", -1, False))
    wide = jnp.concatenate([inner, wide, outer], axis=3)
    wide_shifts = jnp.concatenate([inner_shift, shifts, outer_shift], axis=1)
    return wide, wide_shifts


def rotate_window(window, offsets, out_len):
    take = SMAX - offsets
    nbits = SMAX.bit_length()
    spare = (1 << nbits) - 1 + out_len - window.shape[2]
    if spare > 0:
        pad = jnp.zeros(window.shape[:2] + (spare,) + window.shape[3:], window.dtype)
        window = jnp.concatenate([window, pad], axis=2)
    for bit in range(nbits):
        amount = 1 << bit
        length = window.shape[2] - amount
        chosen = take // amount % 2 == 1
        window = jnp.where(
            chosen[None, None, None, :], window[:, :, amount:], window[:, :, :length]
        )
    return window[:, :, :out_len]


def relay_seat(lane, source, plane, blocks):
    if source // 2 == lane:
        return source
    if 2 * lane + 1 < plane - blocks and 2 * lane < blocks:
        return 2 * lane + 1
    return 2 * lane


def crossing_relays(groups, count, plane, blocks):
    half = plane // 2
    first, second = [], []
    for g in range(groups):
        for block in range(count // plane):
            base = block * plane
            after = (base + plane) % count
            for j in range(1, blocks + 1):
                lane = (3 * g + j - 1) % half
                relay = base + relay_seat(lane, plane - j, plane, blocks)
                first.append((g * count + base + plane - j, g * count + relay))
                second.append((g * count + relay, g * count + after + blocks - j))
    return first, second


def rotation_pieces(head, plane, blocks):
    count = lax.axis_size("azi")
    groups = lax.axis_size("rad")
    if count % plane or count <= plane or plane < 2 * blocks:
        return [passed_along(head, "azi", k) for k in range(1, blocks + 1)]
    near = []
    for k in range(1, blocks + 1):
        pairs = [
            (a, (a + k) % count)
            for a in range(count)
            if a // plane == ((a + k) % count) // plane
        ]
        near.append(lax.ppermute(head, "azi", pairs))
    first, second = crossing_relays(groups, count, plane, blocks)
    relayed = lax.ppermute(head, ("rad", "azi"), first)
    crossed = lax.ppermute(relayed, ("rad", "azi"), second)
    position = lax.axis_index("azi") % plane
    pieces = []
    for k in range(1, blocks + 1):
        if k == blocks:
            far = crossed
        else:
            t = blocks - k
            pairs = [
                (base + i + t, base + i)
                for base in range(0, count, plane)
                for i in range(blocks - t)
            ]
            far = lax.ppermute(crossed, "azi", pairs)
        pieces.append(jnp.where(position < k, far, near[k - 1]))
    return pieces


def local(fields, shifts):
    cells = fields.shape[2]
    rows = fields.shape[3]
    total_rows = rows * lax.axis_size("rad")
    width = STEPS
    wide, wide_shifts = halo_exchange(fields, shifts, width)
    start_row = lax.axis_index("rad") * rows
    blocks = (SMAX + cells - 1) // cells
    for step in range(STEPS):
        w = width - step
        row_index = start_row - w + jnp.arange(rows + 2 * w, dtype=jnp.int32)
        inside = (row_index >= 0) & (row_index < total_rows)
        wide = jnp.where(inside[None, None, None, :], wide, 0.0)
        inner_rows = row_index[1:-1]
        radius = 1.0 + (inner_rows.astype(jnp.float32) + 0.5) / jnp.float32(total_rows)
        inverse = 1.0 / radius
        updated = update(wide, inverse)
        a = w - 1
        head = updated[:, :, :cells]
        pieces = rotation_pieces(head, PLANE, blocks)
        window = jnp.concatenate(pieces[::-1] + [updated], axis=2)
        window = window[:, :, blocks * cells - SMAX :]
        wide_shifts = wide_shifts[:, 1:-1]
        wide = rotate_window(window, wide_shifts[step], cells + 2 * a)
    return wide


def solution(mesh):
    placed = (P(None, None, "azi", "rad"), P(None, "rad"))
    return jax.shard_map(
        local, mesh=mesh, in_specs=placed, out_specs=P(None, None, "azi", "rad"), check_vma=False
    )
```

```python
import jax
import jax.numpy as jnp
from jax import lax
from jax.sharding import PartitionSpec as P

STEPS = 3
SMAX = 192
PLANE = 16
GROUP = 4


courant = 0.2
viscous = 0.1


def passed_along(value, axis, steps, wrap=True):
    count = lax.axis_size(axis)
    if wrap:
        pairs = [(source, (source + steps) % count) for source in range(count)]
    else:
        pairs = [
            (source, source + steps)
            for source in range(count)
            if 0 <= source + steps < count
        ]
    return lax.ppermute(value, axis, pairs)


def update(padded, inverse):
    centre = padded[:, :, 1:-1, 1:-1]
    inner = padded[:, :, 1:-1, :-2]
    outer = padded[:, :, 1:-1, 2:]
    behind = padded[:, :, :-2, 1:-1]
    ahead = padded[:, :, 2:, 1:-1]
    polar_pad = jnp.concatenate([centre[:, :1], centre, centre[:, -1:]], axis=1)
    polar_sum = polar_pad[:, 2:] + polar_pad[:, :-2]
    radial_vel = centre[1]
    azim_vel = centre[2]
    advect = courant * (
        jnp.maximum(radial_vel, 0.0) * (centre - inner)
        + jnp.minimum(radial_vel, 0.0) * (outer - centre)
        + inverse
        * (
            jnp.maximum(azim_vel, 0.0) * (centre - behind)
            + jnp.minimum(azim_vel, 0.0) * (ahead - centre)
        )
    )
    laplace = (
        outer
        + inner
        - 2.0 * centre
        + inverse * inverse * (ahead + behind - 2.0 * centre)
        + (polar_sum - 2.0 * centre)
    )
    radial_diff = (outer - inner) * 0.5
    azim_diff = (ahead - behind) * 0.5
    diverge = radial_diff[1] + inverse * azim_diff[2]
    log_rho = centre[0]
    temper = centre[4]
    new_log = log_rho - advect[0] - courant * diverge
    new_radial = (
        radial_vel
        - advect[1]
        - courant * (temper * radial_diff[0] + radial_diff[4])
        + 0.5 * courant * inverse * azim_vel * azim_vel
        + viscous * laplace[1]
    )
    new_azim = (
        azim_vel
        - advect[2]
        - courant * inverse * (temper * azim_diff[0] + azim_diff[4])
        - 0.5 * courant * inverse * radial_vel * azim_vel
        + viscous * laplace[2]
    )
    new_polar = centre[3] - advect[3] + viscous * laplace[3]
    new_temper = temper - advect[4] - courant * 0.4 * temper * diverge + viscous * laplace[4]
    return jnp.stack([new_log, new_radial, new_azim, new_polar, new_temper])


def halo_exchange(fields, shifts, width):
    cells = fields.shape[2]
    last = fields[:, :, cells - width :]
    first = fields[:, :, :width]
    before = passed_along(last, "azi", 1)
    after = passed_along(first, "azi", -1)
    wide = jnp.concatenate([before, fields, after], axis=2)

    rows = wide.shape[3]
    shape = wide.shape[:3] + (width,)
    count = shape[0] * shape[1] * shape[2] * shape[3]

    def pack(lo, hi):
        part = wide[:, :, :, lo:hi].reshape(-1)
        rates = shifts[:, lo:hi].astype(jnp.float32).reshape(-1)
        return jnp.concatenate([part, rates])

    def unpack(flat):
        part = flat[:count].reshape(shape)
        rates = flat[count:].reshape(shifts.shape[0], width)
        return part, rates.astype(jnp.int32)

    inner, inner_shift = unpack(passed_along(pack(rows - width, rows), "rad", 1, False))
    outer, outer_shift = unpack(passed_along(pack(0, width), "rad", -1, False))
    wide = jnp.concatenate([inner, wide, outer], axis=3)
    wide_shifts = jnp.concatenate([inner_shift, shifts, outer_shift], axis=1)
    return wide, wide_shifts


def rotate_window(window, offsets, out_len):
    take = SMAX - offsets
    nbits = SMAX.bit_length()
    spare = (1 << nbits) - 1 + out_len - window.shape[2]
    if spare > 0:
        pad = jnp.zeros(window.shape[:2] + (spare,) + window.shape[3:], window.dtype)
        window = jnp.concatenate([window, pad], axis=2)
    for bit in range(nbits):
        amount = 1 << bit
        length = window.shape[2] - amount
        chosen = take // amount % 2 == 1
        window = jnp.where(
            chosen[None, None, None, :], window[:, :, amount:], window[:, :, :length]
        )
    return window[:, :, :out_len]


def relay_seat(lane, source, plane, blocks):
    if source // 2 == lane:
        return source
    if 2 * lane + 1 < plane - blocks and 2 * lane < blocks:
        return 2 * lane + 1
    return 2 * lane


def crossing_relays(groups, count, plane, blocks):
    half = plane // 2
    first, second = [], []
    for g in range(groups):
        for block in range(count // plane):
            base = block * plane
            after = (base + plane) % count
            for j in range(1, blocks + 1):
                lane = (3 * g + j - 1) % half
                relay = base + relay_seat(lane, plane - j, plane, blocks)
                first.append((g * count + base + plane - j, g * count + relay))
                second.append((g * count + relay, g * count + after + blocks - j))
    return first, second


def rotation_pieces(head, plane, blocks):
    count = lax.axis_size("azi")
    groups = lax.axis_size("rad")
    if count % plane or count <= plane or plane < 2 * blocks:
        return [passed_along(head, "azi", k) for k in range(1, blocks + 1)]
    near = []
    for k in range(1, blocks + 1):
        pairs = [
            (a, (a + k) % count)
            for a in range(count)
            if a // plane == ((a + k) % count) // plane
        ]
        near.append(lax.ppermute(head, "azi", pairs))
    first, second = crossing_relays(groups, count, plane, blocks)
    relayed = lax.ppermute(head, ("rad", "azi"), first)
    crossed = lax.ppermute(relayed, ("rad", "azi"), second)
    position = lax.axis_index("azi") % plane
    pieces = []
    for k in range(1, blocks + 1):
        if k == blocks:
            far = crossed
        else:
            t = blocks - k
            pairs = [
                (base + i + t, base + i)
                for base in range(0, count, plane)
                for i in range(blocks - t)
            ]
            far = lax.ppermute(crossed, "azi", pairs)
        pieces.append(jnp.where(position < k, far, near[k - 1]))
    return pieces


def in_group(value, delta, group):
    count = lax.axis_size("azi")
    pairs = [(a, a - a % group + (a % group + delta) % group) for a in range(count)]
    return lax.ppermute(value, "azi", pairs)


def by_source(received, seat, group):
    stacked = jnp.stack(received)
    return [
        lax.dynamic_index_in_dim(stacked, (seat - p) % group, keepdims=False)
        for p in range(group)
    ]


def regroup(wide, wide_shifts, cells, rows, width, group):
    seat = lax.axis_index("azi") % group
    part = rows // group
    span = part + 2 * width
    received = []
    for delta in range(group):
        target = (seat + delta) % group
        piece = lax.dynamic_slice_in_dim(wide, target * part, span, axis=3)
        received.append(piece if delta == 0 else in_group(piece, delta, group))
    pieces = by_source(received, seat, group)
    cut = [pieces[0][:, :, : cells + width]]
    cut += [p[:, :, width : cells + width] for p in pieces[1:-1]]
    cut.append(pieces[-1][:, :, width:])
    grouped = jnp.concatenate(cut, axis=2)
    grouped_shifts = lax.dynamic_slice_in_dim(wide_shifts, seat * part, span, axis=1)
    return grouped, grouped_shifts


def ungroup(out, cells, group):
    seat = lax.axis_index("azi") % group
    received = []
    for delta in range(group):
        target = (seat + delta) % group
        piece = lax.dynamic_slice_in_dim(out, target * cells, cells, axis=2)
        received.append(piece if delta == 0 else in_group(piece, delta, group))
    return jnp.concatenate(by_source(received, seat, group), axis=3)


def local(fields, shifts):
    cells = fields.shape[2]
    rows = fields.shape[3]
    count = lax.axis_size("azi")
    total_rows = rows * lax.axis_size("rad")
    width = STEPS
    wide, wide_shifts = halo_exchange(fields, shifts, width)
    group = GROUP
    if count % group or rows % group or group * cells < SMAX:
        group = 1
    start_row = lax.axis_index("rad") * rows
    if group > 1:
        wide, wide_shifts = regroup(wide, wide_shifts, cells, rows, width, group)
        start_row = start_row + lax.axis_index("azi") % group * (rows // group)
    span = cells * group
    sub_rows = rows // group
    blocks = (SMAX + span - 1) // span
    for step in range(STEPS):
        w = width - step
        row_index = start_row - w + jnp.arange(sub_rows + 2 * w, dtype=jnp.int32)
        inside = (row_index >= 0) & (row_index < total_rows)
        wide = jnp.where(inside[None, None, None, :], wide, 0.0)
        inner_rows = row_index[1:-1]
        radius = 1.0 + (inner_rows.astype(jnp.float32) + 0.5) / jnp.float32(total_rows)
        inverse = 1.0 / radius
        updated = update(wide, inverse)
        a = w - 1
        if group > 1:
            head = updated[:, :, blocks * span - SMAX : span]
            pieces = [passed_along(head, "azi", group * k) for k in range(1, blocks + 1)]
            window = jnp.concatenate(pieces[::-1] + [updated], axis=2)
        else:
            head = updated[:, :, :span]
            pieces = rotation_pieces(head, PLANE, blocks)
            window = jnp.concatenate(pieces[::-1] + [updated], axis=2)
            window = window[:, :, blocks * span - SMAX :]
        wide_shifts = wide_shifts[:, 1:-1]
        wide = rotate_window(window, wide_shifts[step], span + 2 * a)
    if group > 1:
        wide = ungroup(wide, cells, group)
    return wide


def solution(mesh):
    placed = (P(None, None, "azi", "rad"), P(None, "rad"))
    return jax.shard_map(
        local, mesh=mesh, in_specs=placed, out_specs=P(None, None, "azi", "rad"), check_vma=False
    )
```

```python
import jax
import jax.numpy as jnp
from jax import lax
from jax.sharding import PartitionSpec as P

STEPS = 3
SMAX = 192
PLANE = 16
GROUP = 4


courant = 0.2
viscous = 0.1


def passed_along(value, axis, steps, wrap=True):
    count = lax.axis_size(axis)
    if wrap:
        pairs = [(source, (source + steps) % count) for source in range(count)]
    else:
        pairs = [
            (source, source + steps)
            for source in range(count)
            if 0 <= source + steps < count
        ]
    return lax.ppermute(value, axis, pairs)


def update(padded, inverse, cells_last=False):
    centre = padded[:, :, 1:-1, 1:-1]
    if cells_last:
        inner = padded[:, :, :-2, 1:-1]
        outer = padded[:, :, 2:, 1:-1]
        behind = padded[:, :, 1:-1, :-2]
        ahead = padded[:, :, 1:-1, 2:]
        inverse = inverse[:, None]
    else:
        inner = padded[:, :, 1:-1, :-2]
        outer = padded[:, :, 1:-1, 2:]
        behind = padded[:, :, :-2, 1:-1]
        ahead = padded[:, :, 2:, 1:-1]
    polar_pad = jnp.concatenate([centre[:, :1], centre, centre[:, -1:]], axis=1)
    polar_sum = polar_pad[:, 2:] + polar_pad[:, :-2]
    radial_vel = centre[1]
    azim_vel = centre[2]
    advect = courant * (
        jnp.maximum(radial_vel, 0.0) * (centre - inner)
        + jnp.minimum(radial_vel, 0.0) * (outer - centre)
        + inverse
        * (
            jnp.maximum(azim_vel, 0.0) * (centre - behind)
            + jnp.minimum(azim_vel, 0.0) * (ahead - centre)
        )
    )
    laplace = (
        outer
        + inner
        - 2.0 * centre
        + inverse * inverse * (ahead + behind - 2.0 * centre)
        + (polar_sum - 2.0 * centre)
    )
    radial_diff = (outer - inner) * 0.5
    azim_diff = (ahead - behind) * 0.5
    diverge = radial_diff[1] + inverse * azim_diff[2]
    log_rho = centre[0]
    temper = centre[4]
    new_log = log_rho - advect[0] - courant * diverge
    new_radial = (
        radial_vel
        - advect[1]
        - courant * (temper * radial_diff[0] + radial_diff[4])
        + 0.5 * courant * inverse * azim_vel * azim_vel
        + viscous * laplace[1]
    )
    new_azim = (
        azim_vel
        - advect[2]
        - courant * inverse * (temper * azim_diff[0] + azim_diff[4])
        - 0.5 * courant * inverse * radial_vel * azim_vel
        + viscous * laplace[2]
    )
    new_polar = centre[3] - advect[3] + viscous * laplace[3]
    new_temper = temper - advect[4] - courant * 0.4 * temper * diverge + viscous * laplace[4]
    return jnp.stack([new_log, new_radial, new_azim, new_polar, new_temper])


def halo_exchange(fields, shifts, width):
    cells = fields.shape[2]
    last = fields[:, :, cells - width :]
    first = fields[:, :, :width]
    before = passed_along(last, "azi", 1)
    after = passed_along(first, "azi", -1)
    wide = jnp.concatenate([before, fields, after], axis=2)

    rows = wide.shape[3]
    shape = wide.shape[:3] + (width,)
    count = shape[0] * shape[1] * shape[2] * shape[3]

    def pack(lo, hi):
        part = wide[:, :, :, lo:hi].reshape(-1)
        rates = shifts[:, lo:hi].astype(jnp.float32).reshape(-1)
        return jnp.concatenate([part, rates])

    def unpack(flat):
        part = flat[:count].reshape(shape)
        rates = flat[count:].reshape(shifts.shape[0], width)
        return part, rates.astype(jnp.int32)

    inner, inner_shift = unpack(passed_along(pack(rows - width, rows), "rad", 1, False))
    outer, outer_shift = unpack(passed_along(pack(0, width), "rad", -1, False))
    wide = jnp.concatenate([inner, wide, outer], axis=3)
    wide_shifts = jnp.concatenate([inner_shift, shifts, outer_shift], axis=1)
    return wide, wide_shifts


def rotate_window(window, offsets, out_len, axis=2):
    take = SMAX - offsets
    nbits = SMAX.bit_length()
    spare = (1 << nbits) - 1 + out_len - window.shape[axis]
    if spare > 0:
        shape = list(window.shape)
        shape[axis] = spare
        pad = jnp.zeros(shape, window.dtype)
        window = jnp.concatenate([window, pad], axis=axis)
    for bit in range(nbits):
        amount = 1 << bit
        length = window.shape[axis] - amount
        chosen = take // amount % 2 == 1
        chosen = chosen[None, None, None, :] if axis == 2 else chosen[None, None, :, None]
        window = jnp.where(
            chosen,
            lax.slice_in_dim(window, amount, amount + length, axis=axis),
            lax.slice_in_dim(window, 0, length, axis=axis),
        )
    return lax.slice_in_dim(window, 0, out_len, axis=axis)


def relay_seat(lane, source, plane, blocks):
    if source // 2 == lane:
        return source
    if 2 * lane + 1 < plane - blocks and 2 * lane < blocks:
        return 2 * lane + 1
    return 2 * lane


def crossing_relays(groups, count, plane, blocks):
    half = plane // 2
    first, second = [], []
    for g in range(groups):
        for block in range(count // plane):
            base = block * plane
            after = (base + plane) % count
            for j in range(1, blocks + 1):
                lane = (3 * g + j - 1) % half
                relay = base + relay_seat(lane, plane - j, plane, blocks)
                first.append((g * count + base + plane - j, g * count + relay))
                second.append((g * count + relay, g * count + after + blocks - j))
    return first, second


def rotation_pieces(head, plane, blocks):
    count = lax.axis_size("azi")
    groups = lax.axis_size("rad")
    if count % plane or count <= plane or plane < 2 * blocks:
        return [passed_along(head, "azi", k) for k in range(1, blocks + 1)]
    near = []
    for k in range(1, blocks + 1):
        pairs = [
            (a, (a + k) % count)
            for a in range(count)
            if a // plane == ((a + k) % count) // plane
        ]
        near.append(lax.ppermute(head, "azi", pairs))
    first, second = crossing_relays(groups, count, plane, blocks)
    relayed = lax.ppermute(head, ("rad", "azi"), first)
    crossed = lax.ppermute(relayed, ("rad", "azi"), second)
    position = lax.axis_index("azi") % plane
    pieces = []
    for k in range(1, blocks + 1):
        if k == blocks:
            far = crossed
        else:
            t = blocks - k
            pairs = [
                (base + i + t, base + i)
                for base in range(0, count, plane)
                for i in range(blocks - t)
            ]
            far = lax.ppermute(crossed, "azi", pairs)
        pieces.append(jnp.where(position < k, far, near[k - 1]))
    return pieces


def in_group(value, delta, group):
    count = lax.axis_size("azi")
    pairs = [(a, a - a % group + (a % group + delta) % group) for a in range(count)]
    return lax.ppermute(value, "azi", pairs)


def by_source(received, seat, group):
    stacked = jnp.stack(received)
    return [
        lax.dynamic_index_in_dim(stacked, (seat - p) % group, keepdims=False)
        for p in range(group)
    ]


def regroup(wide, wide_shifts, cells, rows, width, group):
    seat = lax.axis_index("azi") % group
    part = rows // group
    span = part + 2 * width
    received = []
    for delta in range(group):
        target = (seat + delta) % group
        piece = lax.dynamic_slice_in_dim(wide, target * part, span, axis=3)
        received.append(piece if delta == 0 else in_group(piece, delta, group))
    pieces = by_source(received, seat, group)
    cut = [pieces[0][:, :, : cells + width]]
    cut += [p[:, :, width : cells + width] for p in pieces[1:-1]]
    cut.append(pieces[-1][:, :, width:])
    grouped = jnp.concatenate(cut, axis=2)
    grouped_shifts = lax.dynamic_slice_in_dim(wide_shifts, seat * part, span, axis=1)
    return grouped, grouped_shifts


def ungroup(out, cells, group):
    seat = lax.axis_index("azi") % group
    received = []
    for delta in range(group):
        target = (seat + delta) % group
        piece = lax.dynamic_slice_in_dim(out, target * cells, cells, axis=2)
        received.append(piece if delta == 0 else in_group(piece, delta, group))
    return jnp.concatenate(by_source(received, seat, group), axis=3)


def local(fields, shifts):
    cells = fields.shape[2]
    rows = fields.shape[3]
    count = lax.axis_size("azi")
    total_rows = rows * lax.axis_size("rad")
    width = STEPS
    wide, wide_shifts = halo_exchange(fields, shifts, width)
    group = GROUP
    if count % group or rows % group or group * cells < SMAX:
        group = 1
    start_row = lax.axis_index("rad") * rows
    if group > 1:
        wide, wide_shifts = regroup(wide, wide_shifts, cells, rows, width, group)
        start_row = start_row + lax.axis_index("azi") % group * (rows // group)
        wide = jnp.swapaxes(wide, 2, 3)
    span = cells * group
    sub_rows = rows // group
    blocks = (SMAX + span - 1) // span
    for step in range(STEPS):
        w = width - step
        row_index = start_row - w + jnp.arange(sub_rows + 2 * w, dtype=jnp.int32)
        inside = (row_index >= 0) & (row_index < total_rows)
        inner_rows = row_index[1:-1]
        radius = 1.0 + (inner_rows.astype(jnp.float32) + 0.5) / jnp.float32(total_rows)
        inverse = 1.0 / radius
        a = w - 1
        if group > 1:
            wide = jnp.where(inside[None, None, :, None], wide, 0.0)
            updated = update(wide, inverse, cells_last=True)
            head = updated[:, :, :, blocks * span - SMAX : span]
            pieces = [passed_along(head, "azi", group * k) for k in range(1, blocks + 1)]
            window = jnp.concatenate(pieces[::-1] + [updated], axis=3)
            wide_shifts = wide_shifts[:, 1:-1]
            wide = rotate_window(window, wide_shifts[step], span + 2 * a, axis=3)
            continue
        wide = jnp.where(inside[None, None, None, :], wide, 0.0)
        updated = update(wide, inverse)
        head = updated[:, :, :span]
        pieces = rotation_pieces(head, PLANE, blocks)
        window = jnp.concatenate(pieces[::-1] + [updated], axis=2)
        window = window[:, :, blocks * span - SMAX :]
        wide_shifts = wide_shifts[:, 1:-1]
        wide = rotate_window(window, wide_shifts[step], span + 2 * a)
    if group > 1:
        wide = ungroup(jnp.swapaxes(wide, 2, 3), cells, group)
    return wide


def solution(mesh):
    placed = (P(None, None, "azi", "rad"), P(None, "rad"))
    return jax.shard_map(
        local, mesh=mesh, in_specs=placed, out_specs=P(None, None, "azi", "rad"), check_vma=False
    )
```

```python
import jax
import jax.numpy as jnp
from jax import lax
from jax.sharding import PartitionSpec as P

STEPS = 3
SMAX = 192
PLANE = 16
GROUP = 4


courant = 0.2
viscous = 0.1


def passed_along(value, axis, steps, wrap=True):
    count = lax.axis_size(axis)
    if wrap:
        pairs = [(source, (source + steps) % count) for source in range(count)]
    else:
        pairs = [
            (source, source + steps)
            for source in range(count)
            if 0 <= source + steps < count
        ]
    return lax.ppermute(value, axis, pairs)


def update(padded, inverse, cells_last=False):
    centre = padded[:, :, 1:-1, 1:-1]
    if cells_last:
        inner = padded[:, :, :-2, 1:-1]
        outer = padded[:, :, 2:, 1:-1]
        behind = padded[:, :, 1:-1, :-2]
        ahead = padded[:, :, 1:-1, 2:]
        inverse = inverse[:, None]
    else:
        inner = padded[:, :, 1:-1, :-2]
        outer = padded[:, :, 1:-1, 2:]
        behind = padded[:, :, :-2, 1:-1]
        ahead = padded[:, :, 2:, 1:-1]
    polar_pad = jnp.concatenate([centre[:, :1], centre, centre[:, -1:]], axis=1)
    polar_sum = polar_pad[:, 2:] + polar_pad[:, :-2]
    radial_vel = centre[1]
    azim_vel = centre[2]
    advect = courant * (
        jnp.maximum(radial_vel, 0.0) * (centre - inner)
        + jnp.minimum(radial_vel, 0.0) * (outer - centre)
        + inverse
        * (
            jnp.maximum(azim_vel, 0.0) * (centre - behind)
            + jnp.minimum(azim_vel, 0.0) * (ahead - centre)
        )
    )
    laplace = (
        outer
        + inner
        - 2.0 * centre
        + inverse * inverse * (ahead + behind - 2.0 * centre)
        + (polar_sum - 2.0 * centre)
    )
    radial_diff = (outer - inner) * 0.5
    azim_diff = (ahead - behind) * 0.5
    diverge = radial_diff[1] + inverse * azim_diff[2]
    log_rho = centre[0]
    temper = centre[4]
    new_log = log_rho - advect[0] - courant * diverge
    new_radial = (
        radial_vel
        - advect[1]
        - courant * (temper * radial_diff[0] + radial_diff[4])
        + 0.5 * courant * inverse * azim_vel * azim_vel
        + viscous * laplace[1]
    )
    new_azim = (
        azim_vel
        - advect[2]
        - courant * inverse * (temper * azim_diff[0] + azim_diff[4])
        - 0.5 * courant * inverse * radial_vel * azim_vel
        + viscous * laplace[2]
    )
    new_polar = centre[3] - advect[3] + viscous * laplace[3]
    new_temper = temper - advect[4] - courant * 0.4 * temper * diverge + viscous * laplace[4]
    return jnp.stack([new_log, new_radial, new_azim, new_polar, new_temper])


def halo_exchange(fields, shifts, width):
    cells = fields.shape[2]
    last = fields[:, :, cells - width :]
    first = fields[:, :, :width]
    before = passed_along(last, "azi", 1)
    after = passed_along(first, "azi", -1)
    wide = jnp.concatenate([before, fields, after], axis=2)

    rows = wide.shape[3]
    shape = wide.shape[:3] + (width,)
    count = shape[0] * shape[1] * shape[2] * shape[3]

    def pack(lo, hi):
        part = wide[:, :, :, lo:hi].reshape(-1)
        rates = shifts[:, lo:hi].astype(jnp.float32).reshape(-1)
        return jnp.concatenate([part, rates])

    def unpack(flat):
        part = flat[:count].reshape(shape)
        rates = flat[count:].reshape(shifts.shape[0], width)
        return part, rates.astype(jnp.int32)

    inner, inner_shift = unpack(passed_along(pack(rows - width, rows), "rad", 1, False))
    outer, outer_shift = unpack(passed_along(pack(0, width), "rad", -1, False))
    wide = jnp.concatenate([inner, wide, outer], axis=3)
    wide_shifts = jnp.concatenate([inner_shift, shifts, outer_shift], axis=1)
    return wide, wide_shifts


def rotate_window(window, offsets, out_len, axis=2):
    take = SMAX - offsets
    nbits = SMAX.bit_length()
    spare = (1 << nbits) - 1 + out_len - window.shape[axis]
    if spare > 0:
        shape = list(window.shape)
        shape[axis] = spare
        pad = jnp.zeros(shape, window.dtype)
        window = jnp.concatenate([window, pad], axis=axis)
    for bit in range(nbits):
        amount = 1 << bit
        length = window.shape[axis] - amount
        chosen = take // amount % 2 == 1
        chosen = chosen[None, None, None, :] if axis == 2 else chosen[None, None, :, None]
        window = jnp.where(
            chosen,
            lax.slice_in_dim(window, amount, amount + length, axis=axis),
            lax.slice_in_dim(window, 0, length, axis=axis),
        )
    return lax.slice_in_dim(window, 0, out_len, axis=axis)


def relay_seat(lane, source, plane, blocks):
    if source // 2 == lane:
        return source
    if 2 * lane + 1 < plane - blocks and 2 * lane < blocks:
        return 2 * lane + 1
    return 2 * lane


def crossing_relays(groups, count, plane, blocks):
    half = plane // 2
    first, second = [], []
    for g in range(groups):
        for block in range(count // plane):
            base = block * plane
            after = (base + plane) % count
            for j in range(1, blocks + 1):
                lane = (3 * g + j - 1) % half
                relay = base + relay_seat(lane, plane - j, plane, blocks)
                first.append((g * count + base + plane - j, g * count + relay))
                second.append((g * count + relay, g * count + after + blocks - j))
    return first, second


def rotation_pieces(head, plane, blocks):
    count = lax.axis_size("azi")
    groups = lax.axis_size("rad")
    if count % plane or count <= plane or plane < 2 * blocks:
        return [passed_along(head, "azi", k) for k in range(1, blocks + 1)]
    near = []
    for k in range(1, blocks + 1):
        pairs = [
            (a, (a + k) % count)
            for a in range(count)
            if a // plane == ((a + k) % count) // plane
        ]
        near.append(lax.ppermute(head, "azi", pairs))
    first, second = crossing_relays(groups, count, plane, blocks)
    relayed = lax.ppermute(head, ("rad", "azi"), first)
    crossed = lax.ppermute(relayed, ("rad", "azi"), second)
    position = lax.axis_index("azi") % plane
    pieces = []
    for k in range(1, blocks + 1):
        if k == blocks:
            far = crossed
        else:
            t = blocks - k
            pairs = [
                (base + i + t, base + i)
                for base in range(0, count, plane)
                for i in range(blocks - t)
            ]
            far = lax.ppermute(crossed, "azi", pairs)
        pieces.append(jnp.where(position < k, far, near[k - 1]))
    return pieces


def in_group(value, delta, group):
    count = lax.axis_size("azi")
    pairs = [(a, a - a % group + (a % group + delta) % group) for a in range(count)]
    return lax.ppermute(value, "azi", pairs)


def by_source(received, seat, group):
    stacked = jnp.stack(received)
    return [
        lax.dynamic_index_in_dim(stacked, (seat - p) % group, keepdims=False)
        for p in range(group)
    ]


def regroup(wide, wide_shifts, cells, rows, width, group):
    seat = lax.axis_index("azi") % group
    part = rows // group
    span = part + 2 * width
    received = []
    for delta in range(group):
        target = (seat + delta) % group
        piece = lax.dynamic_slice_in_dim(wide, target * part, span, axis=3)
        received.append(piece if delta == 0 else in_group(piece, delta, group))
    pieces = by_source(received, seat, group)
    cut = [pieces[0][:, :, : cells + width]]
    cut += [p[:, :, width : cells + width] for p in pieces[1:-1]]
    cut.append(pieces[-1][:, :, width:])
    grouped = jnp.concatenate(cut, axis=2)
    grouped_shifts = lax.dynamic_slice_in_dim(wide_shifts, seat * part, span, axis=1)
    return grouped, grouped_shifts


def ungroup(out, cells, group):
    seat = lax.axis_index("azi") % group
    received = []
    for delta in range(group):
        target = (seat + delta) % group
        piece = lax.dynamic_slice_in_dim(out, target * cells, cells, axis=2)
        received.append(piece if delta == 0 else in_group(piece, delta, group))
    return jnp.concatenate(by_source(received, seat, group), axis=3)


def group_piece(head, group):
    count = lax.axis_size("azi")
    groups = lax.axis_size("rad")
    plane = PLANE
    if count % plane or count <= plane or plane < 4 * group:
        return passed_along(head, "azi", group)
    pairs = [
        (a, (a + group) % count)
        for a in range(count)
        if a // plane == ((a + group) % count) // plane
    ]
    near = lax.ppermute(head, "azi", pairs)
    half = plane // 2
    first, second = [], []
    for g in range(groups):
        for block in range(count // plane):
            base = block * plane
            after = (base + plane) % count
            for q in range(group):
                source = plane - group + q
                lane = (g + 2 * q) % half
                seat = source if source // 2 == lane else 2 * lane + source % 2
                first.append((g * count + base + source, g * count + base + seat))
                second.append((g * count + base + seat, g * count + after + q))
    relayed = lax.ppermute(head, ("rad", "azi"), first)
    crossed = lax.ppermute(relayed, ("rad", "azi"), second)
    position = lax.axis_index("azi") % plane
    return jnp.where(position < group, crossed, near)


def local(fields, shifts):
    cells = fields.shape[2]
    rows = fields.shape[3]
    count = lax.axis_size("azi")
    total_rows = rows * lax.axis_size("rad")
    width = STEPS
    wide, wide_shifts = halo_exchange(fields, shifts, width)
    group = GROUP
    if count % group or rows % group or group * cells < SMAX:
        group = 1
    start_row = lax.axis_index("rad") * rows
    if group > 1:
        wide, wide_shifts = regroup(wide, wide_shifts, cells, rows, width, group)
        start_row = start_row + lax.axis_index("azi") % group * (rows // group)
        wide = jnp.swapaxes(wide, 2, 3)
    span = cells * group
    sub_rows = rows // group
    blocks = (SMAX + span - 1) // span
    for step in range(STEPS):
        w = width - step
        row_index = start_row - w + jnp.arange(sub_rows + 2 * w, dtype=jnp.int32)
        inside = (row_index >= 0) & (row_index < total_rows)
        inner_rows = row_index[1:-1]
        radius = 1.0 + (inner_rows.astype(jnp.float32) + 0.5) / jnp.float32(total_rows)
        inverse = 1.0 / radius
        a = w - 1
        if group > 1:
            wide = jnp.where(inside[None, None, :, None], wide, 0.0)
            updated = update(wide, inverse, cells_last=True)
            head = updated[:, :, :, blocks * span - SMAX : span]
            pieces = [group_piece(head, group)]
            window = jnp.concatenate(pieces[::-1] + [updated], axis=3)
            wide_shifts = wide_shifts[:, 1:-1]
            wide = rotate_window(window, wide_shifts[step], span + 2 * a, axis=3)
            continue
        wide = jnp.where(inside[None, None, None, :], wide, 0.0)
        updated = update(wide, inverse)
        head = updated[:, :, :span]
        pieces = rotation_pieces(head, PLANE, blocks)
        window = jnp.concatenate(pieces[::-1] + [updated], axis=2)
        window = window[:, :, blocks * span - SMAX :]
        wide_shifts = wide_shifts[:, 1:-1]
        wide = rotate_window(window, wide_shifts[step], span + 2 * a)
    if group > 1:
        wide = ungroup(jnp.swapaxes(wide, 2, 3), cells, group)
    return wide


def solution(mesh):
    placed = (P(None, None, "azi", "rad"), P(None, "rad"))
    return jax.shard_map(
        local, mesh=mesh, in_specs=placed, out_specs=P(None, None, "azi", "rad"), check_vma=False
    )
```

```python
import jax
import jax.numpy as jnp
from jax import lax
from jax.sharding import PartitionSpec as P

STEPS = 3
SMAX = 192
PLANE = 16


courant = 0.2
viscous = 0.1


def passed_along(value, axis, steps, wrap=True):
    count = lax.axis_size(axis)
    if wrap:
        pairs = [(source, (source + steps) % count) for source in range(count)]
    else:
        pairs = [
            (source, source + steps)
            for source in range(count)
            if 0 <= source + steps < count
        ]
    return lax.ppermute(value, axis, pairs)


def update(padded, inverse):
    centre = padded[:, :, 1:-1, 1:-1]
    inner = padded[:, :, 1:-1, :-2]
    outer = padded[:, :, 1:-1, 2:]
    behind = padded[:, :, :-2, 1:-1]
    ahead = padded[:, :, 2:, 1:-1]
    polar_pad = jnp.concatenate([centre[:, :1], centre, centre[:, -1:]], axis=1)
    polar_sum = polar_pad[:, 2:] + polar_pad[:, :-2]
    radial_vel = centre[1]
    azim_vel = centre[2]
    advect = courant * (
        jnp.maximum(radial_vel, 0.0) * (centre - inner)
        + jnp.minimum(radial_vel, 0.0) * (outer - centre)
        + inverse
        * (
            jnp.maximum(azim_vel, 0.0) * (centre - behind)
            + jnp.minimum(azim_vel, 0.0) * (ahead - centre)
        )
    )
    laplace = (
        outer
        + inner
        - 2.0 * centre
        + inverse * inverse * (ahead + behind - 2.0 * centre)
        + (polar_sum - 2.0 * centre)
    )
    radial_diff = (outer - inner) * 0.5
    azim_diff = (ahead - behind) * 0.5
    diverge = radial_diff[1] + inverse * azim_diff[2]
    log_rho = centre[0]
    temper = centre[4]
    new_log = log_rho - advect[0] - courant * diverge
    new_radial = (
        radial_vel
        - advect[1]
        - courant * (temper * radial_diff[0] + radial_diff[4])
        + 0.5 * courant * inverse * azim_vel * azim_vel
        + viscous * laplace[1]
    )
    new_azim = (
        azim_vel
        - advect[2]
        - courant * inverse * (temper * azim_diff[0] + azim_diff[4])
        - 0.5 * courant * inverse * radial_vel * azim_vel
        + viscous * laplace[2]
    )
    new_polar = centre[3] - advect[3] + viscous * laplace[3]
    new_temper = temper - advect[4] - courant * 0.4 * temper * diverge + viscous * laplace[4]
    return jnp.stack([new_log, new_radial, new_azim, new_polar, new_temper])


def halo_exchange(fields, shifts, width):
    cells = fields.shape[2]
    last = fields[:, :, cells - width :]
    first = fields[:, :, :width]
    before = passed_along(last, "azi", 1)
    after = passed_along(first, "azi", -1)
    wide = jnp.concatenate([before, fields, after], axis=2)

    rows = wide.shape[3]
    shape = wide.shape[:3] + (width,)
    count = shape[0] * shape[1] * shape[2] * shape[3]

    def pack(lo, hi):
        part = wide[:, :, :, lo:hi].reshape(-1)
        rates = shifts[:, lo:hi].astype(jnp.float32).reshape(-1)
        return jnp.concatenate([part, rates])

    def unpack(flat):
        part = flat[:count].reshape(shape)
        rates = flat[count:].reshape(shifts.shape[0], width)
        return part, rates.astype(jnp.int32)

    inner, inner_shift = unpack(passed_along(pack(rows - width, rows), "rad", 1, False))
    outer, outer_shift = unpack(passed_along(pack(0, width), "rad", -1, False))
    wide = jnp.concatenate([inner, wide, outer], axis=3)
    wide_shifts = jnp.concatenate([inner_shift, shifts, outer_shift], axis=1)
    return wide, wide_shifts


def rotate_window(window, offsets, out_len):
    take = SMAX - offsets
    nbits = SMAX.bit_length()
    spare = (1 << nbits) - 1 + out_len - window.shape[2]
    if spare > 0:
        pad = jnp.zeros(window.shape[:2] + (spare,) + window.shape[3:], window.dtype)
        window = jnp.concatenate([window, pad], axis=2)
    for bit in range(nbits):
        amount = 1 << bit
        length = window.shape[2] - amount
        chosen = take // amount % 2 == 1
        window = jnp.where(
            chosen[None, None, None, :], window[:, :, amount:], window[:, :, :length]
        )
    return window[:, :, :out_len]


def relay_seat(lane, source, plane, blocks):
    if source // 2 == lane:
        return source
    if 2 * lane + 1 < plane - blocks and 2 * lane < blocks:
        return 2 * lane + 1
    return 2 * lane


def crossing_relays(groups, count, plane, blocks):
    half = plane // 2
    first, second = [], []
    for g in range(groups):
        for block in range(count // plane):
            base = block * plane
            after = (base + plane) % count
            for j in range(1, blocks + 1):
                lane = (3 * g + j - 1) % half
                relay = base + relay_seat(lane, plane - j, plane, blocks)
                first.append((g * count + base + plane - j, g * count + relay))
                second.append((g * count + relay, g * count + after + blocks - j))
    return first, second


def rotation_pieces(head, plane, blocks):
    count = lax.axis_size("azi")
    groups = lax.axis_size("rad")
    if count % plane or count <= plane or plane < 2 * blocks:
        return [passed_along(head, "azi", k) for k in range(1, blocks + 1)]
    near = []
    for k in range(1, blocks + 1):
        pairs = [
            (a, (a + k) % count)
            for a in range(count)
            if a // plane == ((a + k) % count) // plane
        ]
        near.append(lax.ppermute(head, "azi", pairs))
    pairs = [
        (base + plane - j, (base + plane) % count + blocks - j)
        for base in range(0, count, plane)
        for j in range(1, blocks + 1)
    ]
    crossed = lax.ppermute(head, "azi", pairs)
    position = lax.axis_index("azi") % plane
    pieces = []
    for k in range(1, blocks + 1):
        if k == blocks:
            far = crossed
        else:
            t = blocks - k
            pairs = [
                (base + i + t, base + i)
                for base in range(0, count, plane)
                for i in range(blocks - t)
            ]
            far = lax.ppermute(crossed, "azi", pairs)
        pieces.append(jnp.where(position < k, far, near[k - 1]))
    return pieces


def local(fields, shifts):
    cells = fields.shape[2]
    rows = fields.shape[3]
    total_rows = rows * lax.axis_size("rad")
    width = STEPS
    wide, wide_shifts = halo_exchange(fields, shifts, width)
    start_row = lax.axis_index("rad") * rows
    blocks = (SMAX + cells - 1) // cells
    for step in range(STEPS):
        w = width - step
        row_index = start_row - w + jnp.arange(rows + 2 * w, dtype=jnp.int32)
        inside = (row_index >= 0) & (row_index < total_rows)
        wide = jnp.where(inside[None, None, None, :], wide, 0.0)
        inner_rows = row_index[1:-1]
        radius = 1.0 + (inner_rows.astype(jnp.float32) + 0.5) / jnp.float32(total_rows)
        inverse = 1.0 / radius
        updated = update(wide, inverse)
        a = w - 1
        head = updated[:, :, :cells]
        pieces = rotation_pieces(head, PLANE, blocks)
        window = jnp.concatenate(pieces[::-1] + [updated], axis=2)
        window = window[:, :, blocks * cells - SMAX :]
        wide_shifts = wide_shifts[:, 1:-1]
        wide = rotate_window(window, wide_shifts[step], cells + 2 * a)
    return wide


def solution(mesh):
    placed = (P(None, None, "azi", "rad"), P(None, "rad"))
    return jax.shard_map(
        local, mesh=mesh, in_specs=placed, out_specs=P(None, None, "azi", "rad"), check_vma=False
    )
```

```python
import jax
import jax.numpy as jnp
from jax import lax
from jax.sharding import PartitionSpec as P

STEPS = 3
SMAX = 192
PLANE = 16
HALVES = 2


courant = 0.2
viscous = 0.1


def passed_along(value, axis, steps, wrap=True):
    count = lax.axis_size(axis)
    if wrap:
        pairs = [(source, (source + steps) % count) for source in range(count)]
    else:
        pairs = [
            (source, source + steps)
            for source in range(count)
            if 0 <= source + steps < count
        ]
    return lax.ppermute(value, axis, pairs)


def update(padded, inverse):
    centre = padded[:, :, 1:-1, 1:-1]
    inner = padded[:, :, 1:-1, :-2]
    outer = padded[:, :, 1:-1, 2:]
    behind = padded[:, :, :-2, 1:-1]
    ahead = padded[:, :, 2:, 1:-1]
    polar_pad = jnp.concatenate([centre[:, :1], centre, centre[:, -1:]], axis=1)
    polar_sum = polar_pad[:, 2:] + polar_pad[:, :-2]
    radial_vel = centre[1]
    azim_vel = centre[2]
    advect = courant * (
        jnp.maximum(radial_vel, 0.0) * (centre - inner)
        + jnp.minimum(radial_vel, 0.0) * (outer - centre)
        + inverse
        * (
            jnp.maximum(azim_vel, 0.0) * (centre - behind)
            + jnp.minimum(azim_vel, 0.0) * (ahead - centre)
        )
    )
    laplace = (
        outer
        + inner
        - 2.0 * centre
        + inverse * inverse * (ahead + behind - 2.0 * centre)
        + (polar_sum - 2.0 * centre)
    )
    radial_diff = (outer - inner) * 0.5
    azim_diff = (ahead - behind) * 0.5
    diverge = radial_diff[1] + inverse * azim_diff[2]
    log_rho = centre[0]
    temper = centre[4]
    new_log = log_rho - advect[0] - courant * diverge
    new_radial = (
        radial_vel
        - advect[1]
        - courant * (temper * radial_diff[0] + radial_diff[4])
        + 0.5 * courant * inverse * azim_vel * azim_vel
        + viscous * laplace[1]
    )
    new_azim = (
        azim_vel
        - advect[2]
        - courant * inverse * (temper * azim_diff[0] + azim_diff[4])
        - 0.5 * courant * inverse * radial_vel * azim_vel
        + viscous * laplace[2]
    )
    new_polar = centre[3] - advect[3] + viscous * laplace[3]
    new_temper = temper - advect[4] - courant * 0.4 * temper * diverge + viscous * laplace[4]
    return jnp.stack([new_log, new_radial, new_azim, new_polar, new_temper])


def halo_exchange(fields, shifts, width):
    cells = fields.shape[2]
    last = fields[:, :, cells - width :]
    first = fields[:, :, :width]
    before = passed_along(last, "azi", 1)
    after = passed_along(first, "azi", -1)
    wide = jnp.concatenate([before, fields, after], axis=2)

    rows = wide.shape[3]
    shape = wide.shape[:3] + (width,)
    count = shape[0] * shape[1] * shape[2] * shape[3]

    def pack(lo, hi):
        part = wide[:, :, :, lo:hi].reshape(-1)
        rates = shifts[:, lo:hi].astype(jnp.float32).reshape(-1)
        return jnp.concatenate([part, rates])

    def unpack(flat):
        part = flat[:count].reshape(shape)
        rates = flat[count:].reshape(shifts.shape[0], width)
        return part, rates.astype(jnp.int32)

    inner, inner_shift = unpack(passed_along(pack(rows - width, rows), "rad", 1, False))
    outer, outer_shift = unpack(passed_along(pack(0, width), "rad", -1, False))
    wide = jnp.concatenate([inner, wide, outer], axis=3)
    wide_shifts = jnp.concatenate([inner_shift, shifts, outer_shift], axis=1)
    return wide, wide_shifts


def rotate_window(window, offsets, out_len):
    take = SMAX - offsets
    nbits = SMAX.bit_length()
    spare = (1 << nbits) - 1 + out_len - window.shape[2]
    if spare > 0:
        pad = jnp.zeros(window.shape[:2] + (spare,) + window.shape[3:], window.dtype)
        window = jnp.concatenate([window, pad], axis=2)
    for bit in range(nbits):
        amount = 1 << bit
        length = window.shape[2] - amount
        chosen = take // amount % 2 == 1
        window = jnp.where(
            chosen[None, None, None, :], window[:, :, amount:], window[:, :, :length]
        )
    return window[:, :, :out_len]


def relay_seat(lane, source, plane, blocks):
    if source // 2 == lane:
        return source
    if 2 * lane + 1 < plane - blocks and 2 * lane < blocks:
        return 2 * lane + 1
    return 2 * lane


def crossing_relays(groups, count, plane, blocks, halves):
    half = plane // 2
    first = [[] for _ in range(halves)]
    second = [[] for _ in range(halves)]
    for g in range(groups):
        for block in range(count // plane):
            base = block * plane
            after = (base + plane) % count
            for j in range(1, blocks + 1):
                for h in range(halves):
                    lane = (3 * g + j - 1 + h * half // halves) % half
                    relay = base + relay_seat(lane, plane - j, plane, blocks)
                    first[h].append((g * count + base + plane - j, g * count + relay))
                    second[h].append((g * count + relay, g * count + after + blocks - j))
    return first, second


def rotation_pieces(head, plane, blocks):
    count = lax.axis_size("azi")
    groups = lax.axis_size("rad")
    if count % plane or count <= plane or plane < 2 * blocks:
        return [passed_along(head, "azi", k) for k in range(1, blocks + 1)]
    near = []
    for k in range(1, blocks + 1):
        pairs = [
            (a, (a + k) % count)
            for a in range(count)
            if a // plane == ((a + k) % count) // plane
        ]
        near.append(lax.ppermute(head, "azi", pairs))
    halves = HALVES if head.shape[2] % HALVES == 0 and plane >= 4 * blocks else 1
    first, second = crossing_relays(groups, count, plane, blocks, halves)
    size = head.shape[2] // halves
    parts = []
    for h in range(halves):
        part = head[:, :, h * size : (h + 1) * size]
        relayed = lax.ppermute(part, ("rad", "azi"), first[h])
        parts.append(lax.ppermute(relayed, ("rad", "azi"), second[h]))
    crossed = jnp.concatenate(parts, axis=2)
    position = lax.axis_index("azi") % plane
    pieces = []
    for k in range(1, blocks + 1):
        if k == blocks:
            far = crossed
        else:
            t = blocks - k
            pairs = [
                (base + i + t, base + i)
                for base in range(0, count, plane)
                for i in range(blocks - t)
            ]
            far = lax.ppermute(crossed, "azi", pairs)
        pieces.append(jnp.where(position < k, far, near[k - 1]))
    return pieces


def local(fields, shifts):
    cells = fields.shape[2]
    rows = fields.shape[3]
    total_rows = rows * lax.axis_size("rad")
    width = STEPS
    wide, wide_shifts = halo_exchange(fields, shifts, width)
    start_row = lax.axis_index("rad") * rows
    blocks = (SMAX + cells - 1) // cells
    for step in range(STEPS):
        w = width - step
        row_index = start_row - w + jnp.arange(rows + 2 * w, dtype=jnp.int32)
        inside = (row_index >= 0) & (row_index < total_rows)
        wide = jnp.where(inside[None, None, None, :], wide, 0.0)
        inner_rows = row_index[1:-1]
        radius = 1.0 + (inner_rows.astype(jnp.float32) + 0.5) / jnp.float32(total_rows)
        inverse = 1.0 / radius
        updated = update(wide, inverse)
        a = w - 1
        head = updated[:, :, :cells]
        pieces = rotation_pieces(head, PLANE, blocks)
        window = jnp.concatenate(pieces[::-1] + [updated], axis=2)
        window = window[:, :, blocks * cells - SMAX :]
        wide_shifts = wide_shifts[:, 1:-1]
        wide = rotate_window(window, wide_shifts[step], cells + 2 * a)
    return wide


def solution(mesh):
    placed = (P(None, None, "azi", "rad"), P(None, "rad"))
    return jax.shard_map(
        local, mesh=mesh, in_specs=placed, out_specs=P(None, None, "azi", "rad"), check_vma=False
    )
```

```python
import jax
import jax.numpy as jnp
from jax import lax
from jax.sharding import PartitionSpec as P

STEPS = 3
SMAX = 192
PLANE = 16


courant = 0.2
viscous = 0.1


def passed_along(value, axis, steps, wrap=True):
    count = lax.axis_size(axis)
    if wrap:
        pairs = [(source, (source + steps) % count) for source in range(count)]
    else:
        pairs = [
            (source, source + steps)
            for source in range(count)
            if 0 <= source + steps < count
        ]
    return lax.ppermute(value, axis, pairs)


def update(padded, inverse):
    centre = padded[:, :, 1:-1, 1:-1]
    inner = padded[:, :, 1:-1, :-2]
    outer = padded[:, :, 1:-1, 2:]
    behind = padded[:, :, :-2, 1:-1]
    ahead = padded[:, :, 2:, 1:-1]
    polar_pad = jnp.concatenate([centre[:, :1], centre, centre[:, -1:]], axis=1)
    polar_sum = polar_pad[:, 2:] + polar_pad[:, :-2]
    radial_vel = centre[1]
    azim_vel = centre[2]
    advect = courant * (
        jnp.maximum(radial_vel, 0.0) * (centre - inner)
        + jnp.minimum(radial_vel, 0.0) * (outer - centre)
        + inverse
        * (
            jnp.maximum(azim_vel, 0.0) * (centre - behind)
            + jnp.minimum(azim_vel, 0.0) * (ahead - centre)
        )
    )
    laplace = (
        outer
        + inner
        - 2.0 * centre
        + inverse * inverse * (ahead + behind - 2.0 * centre)
        + (polar_sum - 2.0 * centre)
    )
    radial_diff = (outer - inner) * 0.5
    azim_diff = (ahead - behind) * 0.5
    diverge = radial_diff[1] + inverse * azim_diff[2]
    log_rho = centre[0]
    temper = centre[4]
    new_log = log_rho - advect[0] - courant * diverge
    new_radial = (
        radial_vel
        - advect[1]
        - courant * (temper * radial_diff[0] + radial_diff[4])
        + 0.5 * courant * inverse * azim_vel * azim_vel
        + viscous * laplace[1]
    )
    new_azim = (
        azim_vel
        - advect[2]
        - courant * inverse * (temper * azim_diff[0] + azim_diff[4])
        - 0.5 * courant * inverse * radial_vel * azim_vel
        + viscous * laplace[2]
    )
    new_polar = centre[3] - advect[3] + viscous * laplace[3]
    new_temper = temper - advect[4] - courant * 0.4 * temper * diverge + viscous * laplace[4]
    return jnp.stack([new_log, new_radial, new_azim, new_polar, new_temper])


def halo_exchange(fields, shifts, width):
    cells = fields.shape[2]
    last = fields[:, :, cells - width :]
    first = fields[:, :, :width]
    before = passed_along(last, "azi", 1)
    after = passed_along(first, "azi", -1)
    wide = jnp.concatenate([before, fields, after], axis=2)

    rows = wide.shape[3]
    shape = wide.shape[:3] + (width,)
    count = shape[0] * shape[1] * shape[2] * shape[3]

    def pack(lo, hi):
        part = wide[:, :, :, lo:hi].reshape(-1)
        rates = shifts[:, lo:hi].astype(jnp.float32).reshape(-1)
        return jnp.concatenate([part, rates])

    def unpack(flat):
        part = flat[:count].reshape(shape)
        rates = flat[count:].reshape(shifts.shape[0], width)
        return part, rates.astype(jnp.int32)

    inner, inner_shift = unpack(passed_along(pack(rows - width, rows), "rad", 1, False))
    outer, outer_shift = unpack(passed_along(pack(0, width), "rad", -1, False))
    wide = jnp.concatenate([inner, wide, outer], axis=3)
    wide_shifts = jnp.concatenate([inner_shift, shifts, outer_shift], axis=1)
    return wide, wide_shifts


def rotate_window(window, offsets, out_len):
    take = SMAX - offsets
    nbits = SMAX.bit_length()
    spare = (1 << nbits) - 1 + out_len - window.shape[2]
    if spare > 0:
        pad = jnp.zeros(window.shape[:2] + (spare,) + window.shape[3:], window.dtype)
        window = jnp.concatenate([window, pad], axis=2)
    for bit in range(nbits):
        amount = 1 << bit
        length = window.shape[2] - amount
        chosen = take // amount % 2 == 1
        window = jnp.where(
            chosen[None, None, None, :], window[:, :, amount:], window[:, :, :length]
        )
    return window[:, :, :out_len]


def relay_seat(lane, source, plane, blocks):
    if source // 2 == lane:
        return source
    if 2 * lane + 1 < plane - blocks and 2 * lane < blocks:
        return 2 * lane + 1
    return 2 * lane


def crossing_relays(groups, count, plane, blocks):
    half = plane // 2
    first, second = [], []
    for g in range(groups):
        for block in range(count // plane):
            base = block * plane
            after = (base + plane) % count
            for j in range(1, blocks + 1):
                lane = (3 * g + j - 1) % half
                relay = base + relay_seat(lane, plane - j, plane, blocks)
                first.append((g * count + base + plane - j, g * count + relay))
                second.append((g * count + relay, g * count + after + blocks - j))
    return first, second


def rotation_pieces(head, plane, blocks):
    count = lax.axis_size("azi")
    groups = lax.axis_size("rad")
    if count % plane or count <= plane or plane < 2 * blocks:
        return [passed_along(head, "azi", k) for k in range(1, blocks + 1)]
    near = []
    for k in range(1, blocks + 1):
        pairs = [
            (a, (a + k) % count)
            for a in range(count)
            if a // plane == ((a + k) % count) // plane
        ]
        near.append(lax.ppermute(head, "azi", pairs))
    first, second = crossing_relays(groups, count, plane, blocks)
    relayed = lax.ppermute(head, ("rad", "azi"), first)
    near, relayed = lax.optimization_barrier((near, relayed))
    crossed = lax.ppermute(relayed, ("rad", "azi"), second)
    position = lax.axis_index("azi") % plane
    pieces = []
    for k in range(1, blocks + 1):
        if k == blocks:
            far = crossed
        else:
            t = blocks - k
            pairs = [
                (base + i + t, base + i)
                for base in range(0, count, plane)
                for i in range(blocks - t)
            ]
            far = lax.ppermute(crossed, "azi", pairs)
        pieces.append(jnp.where(position < k, far, near[k - 1]))
    return pieces


def local(fields, shifts):
    cells = fields.shape[2]
    rows = fields.shape[3]
    total_rows = rows * lax.axis_size("rad")
    width = STEPS
    wide, wide_shifts = halo_exchange(fields, shifts, width)
    start_row = lax.axis_index("rad") * rows
    blocks = (SMAX + cells - 1) // cells
    for step in range(STEPS):
        w = width - step
        row_index = start_row - w + jnp.arange(rows + 2 * w, dtype=jnp.int32)
        inside = (row_index >= 0) & (row_index < total_rows)
        wide = jnp.where(inside[None, None, None, :], wide, 0.0)
        inner_rows = row_index[1:-1]
        radius = 1.0 + (inner_rows.astype(jnp.float32) + 0.5) / jnp.float32(total_rows)
        inverse = 1.0 / radius
        updated = update(wide, inverse)
        a = w - 1
        head = updated[:, :, :cells]
        pieces = rotation_pieces(head, PLANE, blocks)
        window = jnp.concatenate(pieces[::-1] + [updated], axis=2)
        window = window[:, :, blocks * cells - SMAX :]
        wide_shifts = wide_shifts[:, 1:-1]
        wide = rotate_window(window, wide_shifts[step], cells + 2 * a)
    return wide


def solution(mesh):
    placed = (P(None, None, "azi", "rad"), P(None, "rad"))
    return jax.shard_map(
        local, mesh=mesh, in_specs=placed, out_specs=P(None, None, "azi", "rad"), check_vma=False
    )
```

```python
import jax
import jax.numpy as jnp
from jax import lax
from jax.sharding import PartitionSpec as P

STEPS = 3
SMAX = 192
PLANE = 16


courant = 0.2
viscous = 0.1


def passed_along(value, axis, steps, wrap=True):
    count = lax.axis_size(axis)
    if wrap:
        pairs = [(source, (source + steps) % count) for source in range(count)]
    else:
        pairs = [
            (source, source + steps)
            for source in range(count)
            if 0 <= source + steps < count
        ]
    return lax.ppermute(value, axis, pairs)


def update(padded, inverse):
    centre = padded[:, :, 1:-1, 1:-1]
    inner = padded[:, :, 1:-1, :-2]
    outer = padded[:, :, 1:-1, 2:]
    behind = padded[:, :, :-2, 1:-1]
    ahead = padded[:, :, 2:, 1:-1]
    polar_pad = jnp.concatenate([centre[:, :1], centre, centre[:, -1:]], axis=1)
    polar_sum = polar_pad[:, 2:] + polar_pad[:, :-2]
    radial_vel = centre[1]
    azim_vel = centre[2]
    advect = courant * (
        jnp.maximum(radial_vel, 0.0) * (centre - inner)
        + jnp.minimum(radial_vel, 0.0) * (outer - centre)
        + inverse
        * (
            jnp.maximum(azim_vel, 0.0) * (centre - behind)
            + jnp.minimum(azim_vel, 0.0) * (ahead - centre)
        )
    )
    laplace = (
        outer
        + inner
        - 2.0 * centre
        + inverse * inverse * (ahead + behind - 2.0 * centre)
        + (polar_sum - 2.0 * centre)
    )
    radial_diff = (outer - inner) * 0.5
    azim_diff = (ahead - behind) * 0.5
    diverge = radial_diff[1] + inverse * azim_diff[2]
    log_rho = centre[0]
    temper = centre[4]
    new_log = log_rho - advect[0] - courant * diverge
    new_radial = (
        radial_vel
        - advect[1]
        - courant * (temper * radial_diff[0] + radial_diff[4])
        + 0.5 * courant * inverse * azim_vel * azim_vel
        + viscous * laplace[1]
    )
    new_azim = (
        azim_vel
        - advect[2]
        - courant * inverse * (temper * azim_diff[0] + azim_diff[4])
        - 0.5 * courant * inverse * radial_vel * azim_vel
        + viscous * laplace[2]
    )
    new_polar = centre[3] - advect[3] + viscous * laplace[3]
    new_temper = temper - advect[4] - courant * 0.4 * temper * diverge + viscous * laplace[4]
    return jnp.stack([new_log, new_radial, new_azim, new_polar, new_temper])


def halo_exchange(fields, shifts, width):
    cells = fields.shape[2]
    last = fields[:, :, cells - width :]
    first = fields[:, :, :width]
    before = passed_along(last, "azi", 1)
    after = passed_along(first, "azi", -1)
    wide = jnp.concatenate([before, fields, after], axis=2)

    rows = wide.shape[3]
    shape = wide.shape[:3] + (width,)
    count = shape[0] * shape[1] * shape[2] * shape[3]

    def pack(lo, hi):
        part = wide[:, :, :, lo:hi].reshape(-1)
        rates = shifts[:, lo:hi].astype(jnp.float32).reshape(-1)
        return jnp.concatenate([part, rates])

    def unpack(flat):
        part = flat[:count].reshape(shape)
        rates = flat[count:].reshape(shifts.shape[0], width)
        return part, rates.astype(jnp.int32)

    inner, inner_shift = unpack(passed_along(pack(rows - width, rows), "rad", 1, False))
    outer, outer_shift = unpack(passed_along(pack(0, width), "rad", -1, False))
    wide = jnp.concatenate([inner, wide, outer], axis=3)
    wide_shifts = jnp.concatenate([inner_shift, shifts, outer_shift], axis=1)
    return wide, wide_shifts


def rotate_window(window, offsets, out_len):
    take = SMAX - offsets
    nbits = SMAX.bit_length()
    spare = (1 << nbits) - 1 + out_len - window.shape[2]
    if spare > 0:
        pad = jnp.zeros(window.shape[:2] + (spare,) + window.shape[3:], window.dtype)
        window = jnp.concatenate([window, pad], axis=2)
    for bit in range(nbits):
        amount = 1 << bit
        length = window.shape[2] - amount
        chosen = take // amount % 2 == 1
        window = jnp.where(
            chosen[None, None, None, :], window[:, :, amount:], window[:, :, :length]
        )
    return window[:, :, :out_len]


def relay_seat(lane, source, plane, blocks):
    if source // 2 == lane:
        return source
    if 2 * lane + 1 < plane - blocks and 2 * lane < blocks:
        return 2 * lane + 1
    return 2 * lane


def crossing_relays(groups, count, plane, blocks):
    half = plane // 2
    first, second = [], []
    for g in range(groups):
        for block in range(count // plane):
            base = block * plane
            after = (base + plane) % count
            for j in range(1, blocks + 1):
                lane = (3 * g + j - 1) % half
                relay = base + relay_seat(lane, plane - j, plane, blocks)
                first.append((g * count + base + plane - j, g * count + relay))
                second.append((g * count + relay, g * count + after + blocks - j))
    return first, second


def rotation_pieces(head, plane, blocks):
    count = lax.axis_size("azi")
    groups = lax.axis_size("rad")
    if count % plane or count <= plane or plane < 2 * blocks:
        return [passed_along(head, "azi", k) for k in range(1, blocks + 1)]
    first, second = crossing_relays(groups, count, plane, blocks)
    relayed = lax.ppermute(head, ("rad", "azi"), first)
    crossed = lax.ppermute(relayed, ("rad", "azi"), second)
    later, _ = lax.optimization_barrier((head, relayed))
    near = []
    for k in range(1, blocks + 1):
        pairs = [
            (a, (a + k) % count)
            for a in range(count)
            if a // plane == ((a + k) % count) // plane
        ]
        near.append(lax.ppermute(later, "azi", pairs))
    position = lax.axis_index("azi") % plane
    pieces = []
    for k in range(1, blocks + 1):
        if k == blocks:
            far = crossed
        else:
            t = blocks - k
            pairs = [
                (base + i + t, base + i)
                for base in range(0, count, plane)
                for i in range(blocks - t)
            ]
            far = lax.ppermute(crossed, "azi", pairs)
        pieces.append(jnp.where(position < k, far, near[k - 1]))
    return pieces


def local(fields, shifts):
    cells = fields.shape[2]
    rows = fields.shape[3]
    total_rows = rows * lax.axis_size("rad")
    width = STEPS
    wide, wide_shifts = halo_exchange(fields, shifts, width)
    start_row = lax.axis_index("rad") * rows
    blocks = (SMAX + cells - 1) // cells
    for step in range(STEPS):
        w = width - step
        row_index = start_row - w + jnp.arange(rows + 2 * w, dtype=jnp.int32)
        inside = (row_index >= 0) & (row_index < total_rows)
        wide = jnp.where(inside[None, None, None, :], wide, 0.0)
        inner_rows = row_index[1:-1]
        radius = 1.0 + (inner_rows.astype(jnp.float32) + 0.5) / jnp.float32(total_rows)
        inverse = 1.0 / radius
        updated = update(wide, inverse)
        a = w - 1
        head = updated[:, :, :cells]
        pieces = rotation_pieces(head, PLANE, blocks)
        window = jnp.concatenate(pieces[::-1] + [updated], axis=2)
        window = window[:, :, blocks * cells - SMAX :]
        wide_shifts = wide_shifts[:, 1:-1]
        wide = rotate_window(window, wide_shifts[step], cells + 2 * a)
    return wide


def solution(mesh):
    placed = (P(None, None, "azi", "rad"), P(None, "rad"))
    return jax.shard_map(
        local, mesh=mesh, in_specs=placed, out_specs=P(None, None, "azi", "rad"), check_vma=False
    )
```

```python
import jax
import jax.numpy as jnp
from jax import lax
from jax.sharding import PartitionSpec as P

STEPS = 3
SMAX = 192
PLANE = 16


courant = 0.2
viscous = 0.1


def passed_along(value, axis, steps, wrap=True):
    count = lax.axis_size(axis)
    if wrap:
        pairs = [(source, (source + steps) % count) for source in range(count)]
    else:
        pairs = [
            (source, source + steps)
            for source in range(count)
            if 0 <= source + steps < count
        ]
    return lax.ppermute(value, axis, pairs)


def update(padded, inverse):
    centre = padded[:, :, 1:-1, 1:-1]
    inner = padded[:, :, 1:-1, :-2]
    outer = padded[:, :, 1:-1, 2:]
    behind = padded[:, :, :-2, 1:-1]
    ahead = padded[:, :, 2:, 1:-1]
    polar_pad = jnp.concatenate([centre[:, :1], centre, centre[:, -1:]], axis=1)
    polar_sum = polar_pad[:, 2:] + polar_pad[:, :-2]
    radial_vel = centre[1]
    azim_vel = centre[2]
    advect = courant * (
        jnp.maximum(radial_vel, 0.0) * (centre - inner)
        + jnp.minimum(radial_vel, 0.0) * (outer - centre)
        + inverse
        * (
            jnp.maximum(azim_vel, 0.0) * (centre - behind)
            + jnp.minimum(azim_vel, 0.0) * (ahead - centre)
        )
    )
    laplace = (
        outer
        + inner
        - 2.0 * centre
        + inverse * inverse * (ahead + behind - 2.0 * centre)
        + (polar_sum - 2.0 * centre)
    )
    radial_diff = (outer - inner) * 0.5
    azim_diff = (ahead - behind) * 0.5
    diverge = radial_diff[1] + inverse * azim_diff[2]
    log_rho = centre[0]
    temper = centre[4]
    new_log = log_rho - advect[0] - courant * diverge
    new_radial = (
        radial_vel
        - advect[1]
        - courant * (temper * radial_diff[0] + radial_diff[4])
        + 0.5 * courant * inverse * azim_vel * azim_vel
        + viscous * laplace[1]
    )
    new_azim = (
        azim_vel
        - advect[2]
        - courant * inverse * (temper * azim_diff[0] + azim_diff[4])
        - 0.5 * courant * inverse * radial_vel * azim_vel
        + viscous * laplace[2]
    )
    new_polar = centre[3] - advect[3] + viscous * laplace[3]
    new_temper = temper - advect[4] - courant * 0.4 * temper * diverge + viscous * laplace[4]
    return jnp.stack([new_log, new_radial, new_azim, new_polar, new_temper])


def halo_exchange(fields, shifts, width):
    cells = fields.shape[2]
    last = fields[:, :, cells - width :]
    first = fields[:, :, :width]
    before = passed_along(last, "azi", 1)
    after = passed_along(first, "azi", -1)
    wide = jnp.concatenate([before, fields, after], axis=2)

    rows = wide.shape[3]
    shape = wide.shape[:3] + (width,)
    count = shape[0] * shape[1] * shape[2] * shape[3]

    def pack(lo, hi):
        part = wide[:, :, :, lo:hi].reshape(-1)
        rates = shifts[:, lo:hi].astype(jnp.float32).reshape(-1)
        return jnp.concatenate([part, rates])

    def unpack(flat):
        part = flat[:count].reshape(shape)
        rates = flat[count:].reshape(shifts.shape[0], width)
        return part, rates.astype(jnp.int32)

    inner, inner_shift = unpack(passed_along(pack(rows - width, rows), "rad", 1, False))
    outer, outer_shift = unpack(passed_along(pack(0, width), "rad", -1, False))
    wide = jnp.concatenate([inner, wide, outer], axis=3)
    wide_shifts = jnp.concatenate([inner_shift, shifts, outer_shift], axis=1)
    return wide, wide_shifts


def rotate_window(window, offsets, out_len):
    take = SMAX - offsets
    nbits = SMAX.bit_length()
    spare = (1 << nbits) - 1 + out_len - window.shape[2]
    if spare > 0:
        pad = jnp.zeros(window.shape[:2] + (spare,) + window.shape[3:], window.dtype)
        window = jnp.concatenate([window, pad], axis=2)
    for bit in range(nbits):
        amount = 1 << bit
        length = window.shape[2] - amount
        chosen = take // amount % 2 == 1
        window = jnp.where(
            chosen[None, None, None, :], window[:, :, amount:], window[:, :, :length]
        )
    return window[:, :, :out_len]


def relay_seat(lane, source, plane, blocks):
    if source // 2 == lane:
        return source
    if 2 * lane + 1 < plane - blocks and 2 * lane < blocks:
        return 2 * lane + 1
    return 2 * lane


def crossing_relays(groups, count, plane, blocks):
    half = plane // 2
    first, second = [], []
    for g in range(groups):
        for block in range(count // plane):
            base = block * plane
            after = (base + plane) % count
            for j in range(1, blocks + 1):
                lane = (3 * g + j - 1) % half
                relay = base + relay_seat(lane, plane - j, plane, blocks)
                first.append((g * count + base + plane - j, g * count + relay))
                second.append((g * count + relay, g * count + after + blocks - j))
    return first, second


def rotation_pieces(head, plane, blocks):
    count = lax.axis_size("azi")
    groups = lax.axis_size("rad")
    if count % plane or count <= plane or plane < 2 * blocks:
        return [passed_along(head, "azi", k) for k in range(1, blocks + 1)]
    near = []
    for k in range(1, blocks + 1):
        pairs = [
            (a, (a + k) % count)
            for a in range(count)
            if a // plane == ((a + k) % count) // plane
        ]
        near.append(lax.ppermute(head, "azi", pairs))
    first, second = crossing_relays(groups, count, plane, blocks)
    relayed = lax.ppermute(head, ("rad", "azi"), first)
    crossed = lax.ppermute(relayed, ("rad", "azi"), second)
    direct = [
        (a, b - (blocks - 1))
        for a, b in second
        if (b % plane) == blocks - 1
    ]
    first_seat = lax.ppermute(relayed, ("rad", "azi"), direct)
    position = lax.axis_index("azi") % plane
    pieces = []
    for k in range(1, blocks + 1):
        if k == blocks:
            far = crossed
        elif k == 1 and blocks > 1:
            far = first_seat
        else:
            t = blocks - k
            pairs = [
                (base + i + t, base + i)
                for base in range(0, count, plane)
                for i in range(blocks - t)
            ]
            far = lax.ppermute(crossed, "azi", pairs)
        pieces.append(jnp.where(position < k, far, near[k - 1]))
    return pieces


def local(fields, shifts):
    cells = fields.shape[2]
    rows = fields.shape[3]
    total_rows = rows * lax.axis_size("rad")
    width = STEPS
    wide, wide_shifts = halo_exchange(fields, shifts, width)
    start_row = lax.axis_index("rad") * rows
    blocks = (SMAX + cells - 1) // cells
    for step in range(STEPS):
        w = width - step
        row_index = start_row - w + jnp.arange(rows + 2 * w, dtype=jnp.int32)
        inside = (row_index >= 0) & (row_index < total_rows)
        wide = jnp.where(inside[None, None, None, :], wide, 0.0)
        inner_rows = row_index[1:-1]
        radius = 1.0 + (inner_rows.astype(jnp.float32) + 0.5) / jnp.float32(total_rows)
        inverse = 1.0 / radius
        updated = update(wide, inverse)
        a = w - 1
        head = updated[:, :, :cells]
        pieces = rotation_pieces(head, PLANE, blocks)
        window = jnp.concatenate(pieces[::-1] + [updated], axis=2)
        window = window[:, :, blocks * cells - SMAX :]
        wide_shifts = wide_shifts[:, 1:-1]
        wide = rotate_window(window, wide_shifts[step], cells + 2 * a)
    return wide


def solution(mesh):
    placed = (P(None, None, "azi", "rad"), P(None, "rad"))
    return jax.shard_map(
        local, mesh=mesh, in_specs=placed, out_specs=P(None, None, "azi", "rad"), check_vma=False
    )
```

```python
import jax
import jax.numpy as jnp
from jax import lax
from jax.sharding import PartitionSpec as P

STEPS = 3
SMAX = 192
PLANE = 16


courant = 0.2
viscous = 0.1


def passed_along(value, axis, steps, wrap=True):
    count = lax.axis_size(axis)
    if wrap:
        pairs = [(source, (source + steps) % count) for source in range(count)]
    else:
        pairs = [
            (source, source + steps)
            for source in range(count)
            if 0 <= source + steps < count
        ]
    return lax.ppermute(value, axis, pairs)


def update(padded, inverse):
    centre = padded[:, :, 1:-1, 1:-1]
    inner = padded[:, :, 1:-1, :-2]
    outer = padded[:, :, 1:-1, 2:]
    behind = padded[:, :, :-2, 1:-1]
    ahead = padded[:, :, 2:, 1:-1]
    polar_pad = jnp.concatenate([centre[:, :1], centre, centre[:, -1:]], axis=1)
    polar_sum = polar_pad[:, 2:] + polar_pad[:, :-2]
    radial_vel = centre[1]
    azim_vel = centre[2]
    advect = courant * (
        jnp.maximum(radial_vel, 0.0) * (centre - inner)
        + jnp.minimum(radial_vel, 0.0) * (outer - centre)
        + inverse
        * (
            jnp.maximum(azim_vel, 0.0) * (centre - behind)
            + jnp.minimum(azim_vel, 0.0) * (ahead - centre)
        )
    )
    laplace = (
        outer
        + inner
        - 2.0 * centre
        + inverse * inverse * (ahead + behind - 2.0 * centre)
        + (polar_sum - 2.0 * centre)
    )
    radial_diff = (outer - inner) * 0.5
    azim_diff = (ahead - behind) * 0.5
    diverge = radial_diff[1] + inverse * azim_diff[2]
    log_rho = centre[0]
    temper = centre[4]
    new_log = log_rho - advect[0] - courant * diverge
    new_radial = (
        radial_vel
        - advect[1]
        - courant * (temper * radial_diff[0] + radial_diff[4])
        + 0.5 * courant * inverse * azim_vel * azim_vel
        + viscous * laplace[1]
    )
    new_azim = (
        azim_vel
        - advect[2]
        - courant * inverse * (temper * azim_diff[0] + azim_diff[4])
        - 0.5 * courant * inverse * radial_vel * azim_vel
        + viscous * laplace[2]
    )
    new_polar = centre[3] - advect[3] + viscous * laplace[3]
    new_temper = temper - advect[4] - courant * 0.4 * temper * diverge + viscous * laplace[4]
    return jnp.stack([new_log, new_radial, new_azim, new_polar, new_temper])


def halo_exchange(fields, shifts, width):
    cells = fields.shape[2]
    last = fields[:, :, cells - width :]
    first = fields[:, :, :width]
    before = passed_along(last, "azi", 1)
    after = passed_along(first, "azi", -1)
    wide = jnp.concatenate([before, fields, after], axis=2)

    rows = wide.shape[3]
    shape = wide.shape[:3] + (width,)
    count = shape[0] * shape[1] * shape[2] * shape[3]

    def pack(lo, hi):
        part = wide[:, :, :, lo:hi].reshape(-1)
        rates = shifts[:, lo:hi].astype(jnp.float32).reshape(-1)
        return jnp.concatenate([part, rates])

    def unpack(flat):
        part = flat[:count].reshape(shape)
        rates = flat[count:].reshape(shifts.shape[0], width)
        return part, rates.astype(jnp.int32)

    inner, inner_shift = unpack(passed_along(pack(rows - width, rows), "rad", 1, False))
    outer, outer_shift = unpack(passed_along(pack(0, width), "rad", -1, False))
    wide = jnp.concatenate([inner, wide, outer], axis=3)
    wide_shifts = jnp.concatenate([inner_shift, shifts, outer_shift], axis=1)
    return wide, wide_shifts


def rotate_window(window, offsets, out_len):
    take = SMAX - offsets
    nbits = SMAX.bit_length()
    spare = (1 << nbits) - 1 + out_len - window.shape[2]
    if spare > 0:
        pad = jnp.zeros(window.shape[:2] + (spare,) + window.shape[3:], window.dtype)
        window = jnp.concatenate([window, pad], axis=2)
    for bit in range(nbits):
        amount = 1 << bit
        length = window.shape[2] - amount
        chosen = take // amount % 2 == 1
        window = jnp.where(
            chosen[None, None, None, :], window[:, :, amount:], window[:, :, :length]
        )
    return window[:, :, :out_len]


def relay_seat(lane, source, plane, blocks):
    if source // 2 == lane:
        return source
    if 2 * lane + 1 < plane - blocks and 2 * lane < blocks:
        return 2 * lane + 1
    return 2 * lane


def crossing_relays(groups, count, plane, blocks):
    half = plane // 2
    first, second = [], []
    for g in range(groups):
        for block in range(count // plane):
            base = block * plane
            after = (base + plane) % count
            for j in range(1, blocks + 1):
                lane = (3 * g + j - 1) % half
                relay = base + relay_seat(lane, plane - j, plane, blocks)
                first.append((g * count + base + plane - j, g * count + relay))
                second.append((g * count + relay, g * count + after + blocks - j))
    return first, second


def rotation_pieces(head, plane, blocks):
    count = lax.axis_size("azi")
    groups = lax.axis_size("rad")
    if count % plane or count <= plane or plane < 2 * blocks:
        return [passed_along(head, "azi", k) for k in range(1, blocks + 1)]
    near = []
    for k in range(1, blocks + 1):
        pairs = [
            (a, (a + k) % count)
            for a in range(count)
            if a // plane == ((a + k) % count) // plane
        ]
        near.append(lax.ppermute(head, "azi", pairs))
    first, second = crossing_relays(groups, count, plane, blocks)
    relayed = lax.ppermute(head, ("rad", "azi"), first)
    crossed = lax.ppermute(relayed, ("rad", "azi"), second)
    direct = [
        (a, b - (blocks - 1))
        for a, b in second
        if (b % plane) == blocks - 1
    ]
    first_seat = lax.ppermute(relayed, ("rad", "azi"), direct)
    position = lax.axis_index("azi") % plane
    if blocks == 3:
        swap = [(b + s, b + 1 - s) for b in range(0, count, plane) for s in (0, 1)]
        given = jnp.where(position == 0, first_seat, crossed)
        swapped = lax.ppermute(given, "azi", swap)
        fars = [first_seat, swapped, crossed]
        return [jnp.where(position < k, fars[k - 1], near[k - 1]) for k in (1, 2, 3)]
    pieces = []
    for k in range(1, blocks + 1):
        if k == blocks:
            far = crossed
        elif k == 1 and blocks > 1:
            far = first_seat
        else:
            t = blocks - k
            pairs = [
                (base + i + t, base + i)
                for base in range(0, count, plane)
                for i in range(blocks - t)
            ]
            far = lax.ppermute(crossed, "azi", pairs)
        pieces.append(jnp.where(position < k, far, near[k - 1]))
    return pieces


def local(fields, shifts):
    cells = fields.shape[2]
    rows = fields.shape[3]
    total_rows = rows * lax.axis_size("rad")
    width = STEPS
    wide, wide_shifts = halo_exchange(fields, shifts, width)
    start_row = lax.axis_index("rad") * rows
    blocks = (SMAX + cells - 1) // cells
    for step in range(STEPS):
        w = width - step
        row_index = start_row - w + jnp.arange(rows + 2 * w, dtype=jnp.int32)
        inside = (row_index >= 0) & (row_index < total_rows)
        wide = jnp.where(inside[None, None, None, :], wide, 0.0)
        inner_rows = row_index[1:-1]
        radius = 1.0 + (inner_rows.astype(jnp.float32) + 0.5) / jnp.float32(total_rows)
        inverse = 1.0 / radius
        updated = update(wide, inverse)
        a = w - 1
        head = updated[:, :, :cells]
        pieces = rotation_pieces(head, PLANE, blocks)
        window = jnp.concatenate(pieces[::-1] + [updated], axis=2)
        window = window[:, :, blocks * cells - SMAX :]
        wide_shifts = wide_shifts[:, 1:-1]
        wide = rotate_window(window, wide_shifts[step], cells + 2 * a)
    return wide


def solution(mesh):
    placed = (P(None, None, "azi", "rad"), P(None, "rad"))
    return jax.shard_map(
        local, mesh=mesh, in_specs=placed, out_specs=P(None, None, "azi", "rad"), check_vma=False
    )
```

```python
import jax
import jax.numpy as jnp
from jax import lax
from jax.sharding import PartitionSpec as P

STEPS = 3
SMAX = 192
PLANE = 16


courant = 0.2
viscous = 0.1


def passed_along(value, axis, steps, wrap=True):
    count = lax.axis_size(axis)
    if wrap:
        pairs = [(source, (source + steps) % count) for source in range(count)]
    else:
        pairs = [
            (source, source + steps)
            for source in range(count)
            if 0 <= source + steps < count
        ]
    return lax.ppermute(value, axis, pairs)


def update(padded, inverse):
    centre = padded[:, :, 1:-1, 1:-1]
    inner = padded[:, :, 1:-1, :-2]
    outer = padded[:, :, 1:-1, 2:]
    behind = padded[:, :, :-2, 1:-1]
    ahead = padded[:, :, 2:, 1:-1]
    polar_pad = jnp.concatenate([centre[:, :1], centre, centre[:, -1:]], axis=1)
    polar_sum = polar_pad[:, 2:] + polar_pad[:, :-2]
    radial_vel = centre[1]
    azim_vel = centre[2]
    advect = courant * (
        jnp.maximum(radial_vel, 0.0) * (centre - inner)
        + jnp.minimum(radial_vel, 0.0) * (outer - centre)
        + inverse
        * (
            jnp.maximum(azim_vel, 0.0) * (centre - behind)
            + jnp.minimum(azim_vel, 0.0) * (ahead - centre)
        )
    )
    laplace = (
        outer
        + inner
        - 2.0 * centre
        + inverse * inverse * (ahead + behind - 2.0 * centre)
        + (polar_sum - 2.0 * centre)
    )
    radial_diff = (outer - inner) * 0.5
    azim_diff = (ahead - behind) * 0.5
    diverge = radial_diff[1] + inverse * azim_diff[2]
    log_rho = centre[0]
    temper = centre[4]
    new_log = log_rho - advect[0] - courant * diverge
    new_radial = (
        radial_vel
        - advect[1]
        - courant * (temper * radial_diff[0] + radial_diff[4])
        + 0.5 * courant * inverse * azim_vel * azim_vel
        + viscous * laplace[1]
    )
    new_azim = (
        azim_vel
        - advect[2]
        - courant * inverse * (temper * azim_diff[0] + azim_diff[4])
        - 0.5 * courant * inverse * radial_vel * azim_vel
        + viscous * laplace[2]
    )
    new_polar = centre[3] - advect[3] + viscous * laplace[3]
    new_temper = temper - advect[4] - courant * 0.4 * temper * diverge + viscous * laplace[4]
    return jnp.stack([new_log, new_radial, new_azim, new_polar, new_temper])


def halo_exchange(fields, shifts, width):
    cells = fields.shape[2]
    last = fields[:, :, cells - width :]
    first = fields[:, :, :width]
    before = passed_along(last, "azi", 1)
    after = passed_along(first, "azi", -1)
    wide = jnp.concatenate([before, fields, after], axis=2)

    rows = wide.shape[3]
    shape = wide.shape[:3] + (width,)
    count = shape[0] * shape[1] * shape[2] * shape[3]

    def pack(lo, hi):
        part = wide[:, :, :, lo:hi].reshape(-1)
        rates = shifts[:, lo:hi].astype(jnp.float32).reshape(-1)
        return jnp.concatenate([part, rates])

    def unpack(flat):
        part = flat[:count].reshape(shape)
        rates = flat[count:].reshape(shifts.shape[0], width)
        return part, rates.astype(jnp.int32)

    inner, inner_shift = unpack(passed_along(pack(rows - width, rows), "rad", 1, False))
    outer, outer_shift = unpack(passed_along(pack(0, width), "rad", -1, False))
    wide = jnp.concatenate([inner, wide, outer], axis=3)
    wide_shifts = jnp.concatenate([inner_shift, shifts, outer_shift], axis=1)
    return wide, wide_shifts


def rotate_window(window, offsets, out_len):
    take = SMAX - offsets
    nbits = SMAX.bit_length()
    spare = (1 << nbits) - 1 + out_len - window.shape[2]
    if spare > 0:
        pad = jnp.zeros(window.shape[:2] + (spare,) + window.shape[3:], window.dtype)
        window = jnp.concatenate([window, pad], axis=2)
    for bit in range(nbits):
        amount = 1 << bit
        length = window.shape[2] - amount
        chosen = take // amount % 2 == 1
        window = jnp.where(
            chosen[None, None, None, :], window[:, :, amount:], window[:, :, :length]
        )
    return window[:, :, :out_len]


def relay_seat(lane, source, plane, blocks):
    if source // 2 == lane:
        return source
    if 2 < 2 * lane + 1 < plane - blocks and 2 * lane < blocks:
        return 2 * lane + 1
    return 2 * lane


def crossing_relays(groups, count, plane, blocks):
    half = plane // 2
    first, second = [], []
    for g in range(groups):
        for block in range(count // plane):
            base = block * plane
            after = (base + plane) % count
            for j in range(1, blocks + 1):
                lane = (3 * g + j - 1) % half
                relay = base + relay_seat(lane, plane - j, plane, blocks)
                first.append((g * count + base + plane - j, g * count + relay))
                second.append((g * count + relay, g * count + after + blocks - j))
    return first, second


def rotation_pieces(head, plane, blocks):
    count = lax.axis_size("azi")
    groups = lax.axis_size("rad")
    if count % plane or count <= plane or plane < 2 * blocks:
        return [passed_along(head, "azi", k) for k in range(1, blocks + 1)]
    near = []
    for k in range(1, blocks + 1):
        pairs = [
            (a, (a + k) % count)
            for a in range(count)
            if a // plane == ((a + k) % count) // plane
        ]
        near.append(lax.ppermute(head, "azi", pairs))
    first, second = crossing_relays(groups, count, plane, blocks)
    relayed = lax.ppermute(head, ("rad", "azi"), first)
    crossed = lax.ppermute(relayed, ("rad", "azi"), second)
    direct = [
        (a, b - (blocks - 1))
        for a, b in second
        if (b % plane) == blocks - 1
    ]
    first_seat = lax.ppermute(relayed, ("rad", "azi"), direct)
    position = lax.axis_index("azi") % plane
    pieces = []
    for k in range(1, blocks + 1):
        if k == blocks:
            far = crossed
        elif k == 1 and blocks > 1:
            far = first_seat
        else:
            t = blocks - k
            pairs = [
                (base + i + t, base + i)
                for base in range(0, count, plane)
                for i in range(blocks - t)
            ]
            far = lax.ppermute(crossed, "azi", pairs)
        pieces.append(jnp.where(position < k, far, near[k - 1]))
    return pieces


def local(fields, shifts):
    cells = fields.shape[2]
    rows = fields.shape[3]
    total_rows = rows * lax.axis_size("rad")
    width = STEPS
    wide, wide_shifts = halo_exchange(fields, shifts, width)
    start_row = lax.axis_index("rad") * rows
    blocks = (SMAX + cells - 1) // cells
    for step in range(STEPS):
        w = width - step
        row_index = start_row - w + jnp.arange(rows + 2 * w, dtype=jnp.int32)
        inside = (row_index >= 0) & (row_index < total_rows)
        wide = jnp.where(inside[None, None, None, :], wide, 0.0)
        inner_rows = row_index[1:-1]
        radius = 1.0 + (inner_rows.astype(jnp.float32) + 0.5) / jnp.float32(total_rows)
        inverse = 1.0 / radius
        updated = update(wide, inverse)
        a = w - 1
        head = updated[:, :, :cells]
        pieces = rotation_pieces(head, PLANE, blocks)
        window = jnp.concatenate(pieces[::-1] + [updated], axis=2)
        window = window[:, :, blocks * cells - SMAX :]
        wide_shifts = wide_shifts[:, 1:-1]
        wide = rotate_window(window, wide_shifts[step], cells + 2 * a)
    return wide


def solution(mesh):
    placed = (P(None, None, "azi", "rad"), P(None, "rad"))
    return jax.shard_map(
        local, mesh=mesh, in_specs=placed, out_specs=P(None, None, "azi", "rad"), check_vma=False
    )
```

```python
import jax
import jax.numpy as jnp
from jax import lax
from jax.sharding import PartitionSpec as P

STEPS = 3
SMAX = 192
PLANE = 16


courant = 0.2
viscous = 0.1


def passed_along(value, axis, steps, wrap=True):
    count = lax.axis_size(axis)
    if wrap:
        pairs = [(source, (source + steps) % count) for source in range(count)]
    else:
        pairs = [
            (source, source + steps)
            for source in range(count)
            if 0 <= source + steps < count
        ]
    return lax.ppermute(value, axis, pairs)


def update(padded, inverse):
    centre = padded[:, :, 1:-1, 1:-1]
    inner = padded[:, :, 1:-1, :-2]
    outer = padded[:, :, 1:-1, 2:]
    behind = padded[:, :, :-2, 1:-1]
    ahead = padded[:, :, 2:, 1:-1]
    polar_pad = jnp.concatenate([centre[:, :1], centre, centre[:, -1:]], axis=1)
    polar_sum = polar_pad[:, 2:] + polar_pad[:, :-2]
    radial_vel = centre[1]
    azim_vel = centre[2]
    advect = courant * (
        jnp.maximum(radial_vel, 0.0) * (centre - inner)
        + jnp.minimum(radial_vel, 0.0) * (outer - centre)
        + inverse
        * (
            jnp.maximum(azim_vel, 0.0) * (centre - behind)
            + jnp.minimum(azim_vel, 0.0) * (ahead - centre)
        )
    )
    laplace = (
        outer
        + inner
        - 2.0 * centre
        + inverse * inverse * (ahead + behind - 2.0 * centre)
        + (polar_sum - 2.0 * centre)
    )
    radial_diff = (outer - inner) * 0.5
    azim_diff = (ahead - behind) * 0.5
    diverge = radial_diff[1] + inverse * azim_diff[2]
    log_rho = centre[0]
    temper = centre[4]
    new_log = log_rho - advect[0] - courant * diverge
    new_radial = (
        radial_vel
        - advect[1]
        - courant * (temper * radial_diff[0] + radial_diff[4])
        + 0.5 * courant * inverse * azim_vel * azim_vel
        + viscous * laplace[1]
    )
    new_azim = (
        azim_vel
        - advect[2]
        - courant * inverse * (temper * azim_diff[0] + azim_diff[4])
        - 0.5 * courant * inverse * radial_vel * azim_vel
        + viscous * laplace[2]
    )
    new_polar = centre[3] - advect[3] + viscous * laplace[3]
    new_temper = temper - advect[4] - courant * 0.4 * temper * diverge + viscous * laplace[4]
    return jnp.stack([new_log, new_radial, new_azim, new_polar, new_temper])


def halo_exchange(fields, shifts, width):
    cells = fields.shape[2]
    last = fields[:, :, cells - width :]
    first = fields[:, :, :width]
    before = passed_along(last, "azi", 1)
    after = passed_along(first, "azi", -1)
    wide = jnp.concatenate([before, fields, after], axis=2)

    rows = wide.shape[3]
    shape = wide.shape[:3] + (width,)
    count = shape[0] * shape[1] * shape[2] * shape[3]

    def pack(lo, hi):
        part = wide[:, :, :, lo:hi].reshape(-1)
        rates = shifts[:, lo:hi].astype(jnp.float32).reshape(-1)
        return jnp.concatenate([part, rates])

    def unpack(flat):
        part = flat[:count].reshape(shape)
        rates = flat[count:].reshape(shifts.shape[0], width)
        return part, rates.astype(jnp.int32)

    inner, inner_shift = unpack(passed_along(pack(rows - width, rows), "rad", 1, False))
    outer, outer_shift = unpack(passed_along(pack(0, width), "rad", -1, False))
    wide = jnp.concatenate([inner, wide, outer], axis=3)
    wide_shifts = jnp.concatenate([inner_shift, shifts, outer_shift], axis=1)
    return wide, wide_shifts


def rotate_window(window, offsets, out_len):
    take = SMAX - offsets
    nbits = SMAX.bit_length()
    spare = (1 << nbits) - 1 + out_len - window.shape[2]
    if spare > 0:
        pad = jnp.zeros(window.shape[:2] + (spare,) + window.shape[3:], window.dtype)
        window = jnp.concatenate([window, pad], axis=2)
    for bit in range(nbits):
        amount = 1 << bit
        length = window.shape[2] - amount
        chosen = take // amount % 2 == 1
        window = jnp.where(
            chosen[None, None, None, :], window[:, :, amount:], window[:, :, :length]
        )
    return window[:, :, :out_len]


def relay_seat(lane, source, plane, blocks):
    if source // 2 == lane:
        return source
    if 2 * lane + 1 < plane - blocks and 2 * lane < blocks:
        return 2 * lane + 1
    return 2 * lane


def crossing_relays(groups, count, plane, blocks):
    half = plane // 2
    first, second = [], []
    for g in range(groups):
        for block in range(count // plane):
            base = block * plane
            after = (base + plane) % count
            for j in range(1, blocks + 1):
                lane = (3 * g + j - 1) % half
                relay = base + relay_seat(lane, plane - j, plane, blocks)
                first.append((g * count + base + plane - j, g * count + relay))
                second.append((g * count + relay, g * count + after + blocks - j))
    return first, second


def rotation_pieces(head, plane, blocks):
    count = lax.axis_size("azi")
    groups = lax.axis_size("rad")
    if count % plane or count <= plane or plane < 2 * blocks:
        return [passed_along(head, "azi", k) for k in range(1, blocks + 1)]
    near = []
    for k in range(1, blocks + 1):
        pairs = [
            (a, (a + k) % count)
            for a in range(count)
            if a // plane == ((a + k) % count) // plane
        ]
        near.append(lax.ppermute(head, "azi", pairs))
    first, second = crossing_relays(groups, count, plane, blocks)
    relayed = lax.ppermute(head, ("rad", "azi"), first)
    crossed = lax.ppermute(relayed, ("rad", "azi"), second)
    direct = [
        (a, b - (blocks - 1))
        for a, b in second
        if (b % plane) == blocks - 1
    ]
    first_seat = lax.ppermute(relayed, ("rad", "azi"), direct)
    position = lax.axis_index("azi") % plane
    if blocks == 3:
        second_block = [(a, b - 1) for a, b in second if (b % plane) == 1]
        second_seat = lax.ppermute(relayed, ("rad", "azi"), second_block)
        pairs = [(base + 2, base + 1) for base in range(0, count, plane)]
        passed = lax.ppermute(crossed, "azi", pairs)
        middle = jnp.where(position == 0, second_seat, passed)
        fars = [first_seat, middle, crossed]
        return [jnp.where(position < k, fars[k - 1], near[k - 1]) for k in (1, 2, 3)]
    pieces = []
    for k in range(1, blocks + 1):
        if k == blocks:
            far = crossed
        elif k == 1 and blocks > 1:
            far = first_seat
        else:
            t = blocks - k
            pairs = [
                (base + i + t, base + i)
                for base in range(0, count, plane)
                for i in range(blocks - t)
            ]
            far = lax.ppermute(crossed, "azi", pairs)
        pieces.append(jnp.where(position < k, far, near[k - 1]))
    return pieces


def local(fields, shifts):
    cells = fields.shape[2]
    rows = fields.shape[3]
    total_rows = rows * lax.axis_size("rad")
    width = STEPS
    wide, wide_shifts = halo_exchange(fields, shifts, width)
    start_row = lax.axis_index("rad") * rows
    blocks = (SMAX + cells - 1) // cells
    for step in range(STEPS):
        w = width - step
        row_index = start_row - w + jnp.arange(rows + 2 * w, dtype=jnp.int32)
        inside = (row_index >= 0) & (row_index < total_rows)
        wide = jnp.where(inside[None, None, None, :], wide, 0.0)
        inner_rows = row_index[1:-1]
        radius = 1.0 + (inner_rows.astype(jnp.float32) + 0.5) / jnp.float32(total_rows)
        inverse = 1.0 / radius
        updated = update(wide, inverse)
        a = w - 1
        head = updated[:, :, :cells]
        pieces = rotation_pieces(head, PLANE, blocks)
        window = jnp.concatenate(pieces[::-1] + [updated], axis=2)
        window = window[:, :, blocks * cells - SMAX :]
        wide_shifts = wide_shifts[:, 1:-1]
        wide = rotate_window(window, wide_shifts[step], cells + 2 * a)
    return wide


def solution(mesh):
    placed = (P(None, None, "azi", "rad"), P(None, "rad"))
    return jax.shard_map(
        local, mesh=mesh, in_specs=placed, out_specs=P(None, None, "azi", "rad"), check_vma=False
    )
```

```python
import jax
import jax.numpy as jnp
from jax import lax
from jax.sharding import PartitionSpec as P

STEPS = 3
SMAX = 192
PLANE = 16


courant = 0.2
viscous = 0.1


def passed_along(value, axis, steps, wrap=True):
    count = lax.axis_size(axis)
    if wrap:
        pairs = [(source, (source + steps) % count) for source in range(count)]
    else:
        pairs = [
            (source, source + steps)
            for source in range(count)
            if 0 <= source + steps < count
        ]
    return lax.ppermute(value, axis, pairs)


def update(padded, inverse):
    centre = padded[:, :, 1:-1, 1:-1]
    inner = padded[:, :, 1:-1, :-2]
    outer = padded[:, :, 1:-1, 2:]
    behind = padded[:, :, :-2, 1:-1]
    ahead = padded[:, :, 2:, 1:-1]
    polar_pad = jnp.concatenate([centre[:, :1], centre, centre[:, -1:]], axis=1)
    polar_sum = polar_pad[:, 2:] + polar_pad[:, :-2]
    radial_vel = centre[1]
    azim_vel = centre[2]
    advect = courant * (
        jnp.maximum(radial_vel, 0.0) * (centre - inner)
        + jnp.minimum(radial_vel, 0.0) * (outer - centre)
        + inverse
        * (
            jnp.maximum(azim_vel, 0.0) * (centre - behind)
            + jnp.minimum(azim_vel, 0.0) * (ahead - centre)
        )
    )
    laplace = (
        outer
        + inner
        - 2.0 * centre
        + inverse * inverse * (ahead + behind - 2.0 * centre)
        + (polar_sum - 2.0 * centre)
    )
    radial_diff = (outer - inner) * 0.5
    azim_diff = (ahead - behind) * 0.5
    diverge = radial_diff[1] + inverse * azim_diff[2]
    log_rho = centre[0]
    temper = centre[4]
    new_log = log_rho - advect[0] - courant * diverge
    new_radial = (
        radial_vel
        - advect[1]
        - courant * (temper * radial_diff[0] + radial_diff[4])
        + 0.5 * courant * inverse * azim_vel * azim_vel
        + viscous * laplace[1]
    )
    new_azim = (
        azim_vel
        - advect[2]
        - courant * inverse * (temper * azim_diff[0] + azim_diff[4])
        - 0.5 * courant * inverse * radial_vel * azim_vel
        + viscous * laplace[2]
    )
    new_polar = centre[3] - advect[3] + viscous * laplace[3]
    new_temper = temper - advect[4] - courant * 0.4 * temper * diverge + viscous * laplace[4]
    return jnp.stack([new_log, new_radial, new_azim, new_polar, new_temper])


def halo_exchange(fields, shifts, width):
    cells = fields.shape[2]
    last = fields[:, :, cells - width :]
    first = fields[:, :, :width]
    before = passed_along(last, "azi", 1)
    after = passed_along(first, "azi", -1)
    wide = jnp.concatenate([before, fields, after], axis=2)

    rows = wide.shape[3]
    shape = wide.shape[:3] + (width,)
    count = shape[0] * shape[1] * shape[2] * shape[3]

    def pack(lo, hi):
        part = wide[:, :, :, lo:hi].reshape(-1)
        rates = shifts[:, lo:hi].astype(jnp.float32).reshape(-1)
        return jnp.concatenate([part, rates])

    def unpack(flat):
        part = flat[:count].reshape(shape)
        rates = flat[count:].reshape(shifts.shape[0], width)
        return part, rates.astype(jnp.int32)

    inner, inner_shift = unpack(passed_along(pack(rows - width, rows), "rad", 1, False))
    outer, outer_shift = unpack(passed_along(pack(0, width), "rad", -1, False))
    wide = jnp.concatenate([inner, wide, outer], axis=3)
    wide_shifts = jnp.concatenate([inner_shift, shifts, outer_shift], axis=1)
    return wide, wide_shifts


def rotate_window(window, offsets, out_len):
    take = SMAX - offsets
    nbits = SMAX.bit_length()
    spare = (1 << nbits) - 1 + out_len - window.shape[2]
    if spare > 0:
        pad = jnp.zeros(window.shape[:2] + (spare,) + window.shape[3:], window.dtype)
        window = jnp.concatenate([window, pad], axis=2)
    for bit in range(nbits):
        amount = 1 << bit
        length = window.shape[2] - amount
        chosen = take // amount % 2 == 1
        window = jnp.where(
            chosen[None, None, None, :], window[:, :, amount:], window[:, :, :length]
        )
    return window[:, :, :out_len]


def relay_seat(lane, source, plane, blocks):
    if source // 2 == lane:
        return source
    if 2 * lane + 1 < plane - blocks and 2 * lane < blocks:
        return 2 * lane + 1
    return 2 * lane


def crossing_relays(groups, count, plane, blocks):
    half = plane // 2
    first, second = [], []
    for g in range(groups):
        for block in range(count // plane):
            base = block * plane
            after = (base + plane) % count
            for j in range(1, blocks + 1):
                lane = (3 * g + j + 3) % half
                relay = base + relay_seat(lane, plane - j, plane, blocks)
                first.append((g * count + base + plane - j, g * count + relay))
                second.append((g * count + relay, g * count + after + blocks - j))
    return first, second


def rotation_pieces(head, plane, blocks):
    count = lax.axis_size("azi")
    groups = lax.axis_size("rad")
    if count % plane or count <= plane or plane < 2 * blocks:
        return [passed_along(head, "azi", k) for k in range(1, blocks + 1)]
    near = []
    for k in range(1, blocks + 1):
        pairs = [
            (a, (a + k) % count)
            for a in range(count)
            if a // plane == ((a + k) % count) // plane
        ]
        near.append(lax.ppermute(head, "azi", pairs))
    first, second = crossing_relays(groups, count, plane, blocks)
    relayed = lax.ppermute(head, ("rad", "azi"), first)
    crossed = lax.ppermute(relayed, ("rad", "azi"), second)
    direct = [
        (a, b - (blocks - 1))
        for a, b in second
        if (b % plane) == blocks - 1
    ]
    first_seat = lax.ppermute(relayed, ("rad", "azi"), direct)
    position = lax.axis_index("azi") % plane
    pieces = []
    for k in range(1, blocks + 1):
        if k == blocks:
            far = crossed
        elif k == 1 and blocks > 1:
            far = first_seat
        else:
            t = blocks - k
            pairs = [
                (base + i + t, base + i)
                for base in range(0, count, plane)
                for i in range(blocks - t)
            ]
            far = lax.ppermute(crossed, "azi", pairs)
        pieces.append(jnp.where(position < k, far, near[k - 1]))
    return pieces


def local(fields, shifts):
    cells = fields.shape[2]
    rows = fields.shape[3]
    total_rows = rows * lax.axis_size("rad")
    width = STEPS
    wide, wide_shifts = halo_exchange(fields, shifts, width)
    start_row = lax.axis_index("rad") * rows
    blocks = (SMAX + cells - 1) // cells
    for step in range(STEPS):
        w = width - step
        row_index = start_row - w + jnp.arange(rows + 2 * w, dtype=jnp.int32)
        inside = (row_index >= 0) & (row_index < total_rows)
        wide = jnp.where(inside[None, None, None, :], wide, 0.0)
        inner_rows = row_index[1:-1]
        radius = 1.0 + (inner_rows.astype(jnp.float32) + 0.5) / jnp.float32(total_rows)
        inverse = 1.0 / radius
        updated = update(wide, inverse)
        a = w - 1
        head = updated[:, :, :cells]
        pieces = rotation_pieces(head, PLANE, blocks)
        window = jnp.concatenate(pieces[::-1] + [updated], axis=2)
        window = window[:, :, blocks * cells - SMAX :]
        wide_shifts = wide_shifts[:, 1:-1]
        wide = rotate_window(window, wide_shifts[step], cells + 2 * a)
    return wide


def solution(mesh):
    placed = (P(None, None, "azi", "rad"), P(None, "rad"))
    return jax.shard_map(
        local, mesh=mesh, in_specs=placed, out_specs=P(None, None, "azi", "rad"), check_vma=False
    )
```

```python
import jax
import jax.numpy as jnp
from jax import lax
from jax.sharding import PartitionSpec as P

STEPS = 3
SMAX = 192
PLANE = 16


courant = 0.2
viscous = 0.1


def passed_along(value, axis, steps, wrap=True):
    count = lax.axis_size(axis)
    if wrap:
        pairs = [(source, (source + steps) % count) for source in range(count)]
    else:
        pairs = [
            (source, source + steps)
            for source in range(count)
            if 0 <= source + steps < count
        ]
    return lax.ppermute(value, axis, pairs)


def update(padded, inverse):
    centre = padded[:, :, 1:-1, 1:-1]
    inner = padded[:, :, 1:-1, :-2]
    outer = padded[:, :, 1:-1, 2:]
    behind = padded[:, :, :-2, 1:-1]
    ahead = padded[:, :, 2:, 1:-1]
    polar_pad = jnp.concatenate([centre[:, :1], centre, centre[:, -1:]], axis=1)
    polar_sum = polar_pad[:, 2:] + polar_pad[:, :-2]
    radial_vel = centre[1]
    azim_vel = centre[2]
    advect = courant * (
        jnp.maximum(radial_vel, 0.0) * (centre - inner)
        + jnp.minimum(radial_vel, 0.0) * (outer - centre)
        + inverse
        * (
            jnp.maximum(azim_vel, 0.0) * (centre - behind)
            + jnp.minimum(azim_vel, 0.0) * (ahead - centre)
        )
    )
    laplace = (
        outer
        + inner
        - 2.0 * centre
        + inverse * inverse * (ahead + behind - 2.0 * centre)
        + (polar_sum - 2.0 * centre)
    )
    radial_diff = (outer - inner) * 0.5
    azim_diff = (ahead - behind) * 0.5
    diverge = radial_diff[1] + inverse * azim_diff[2]
    log_rho = centre[0]
    temper = centre[4]
    new_log = log_rho - advect[0] - courant * diverge
    new_radial = (
        radial_vel
        - advect[1]
        - courant * (temper * radial_diff[0] + radial_diff[4])
        + 0.5 * courant * inverse * azim_vel * azim_vel
        + viscous * laplace[1]
    )
    new_azim = (
        azim_vel
        - advect[2]
        - courant * inverse * (temper * azim_diff[0] + azim_diff[4])
        - 0.5 * courant * inverse * radial_vel * azim_vel
        + viscous * laplace[2]
    )
    new_polar = centre[3] - advect[3] + viscous * laplace[3]
    new_temper = temper - advect[4] - courant * 0.4 * temper * diverge + viscous * laplace[4]
    return jnp.stack([new_log, new_radial, new_azim, new_polar, new_temper])


def halo_exchange(fields, shifts, width):
    cells = fields.shape[2]
    last = fields[:, :, cells - width :]
    first = fields[:, :, :width]
    before = passed_along(last, "azi", 1)
    after = passed_along(first, "azi", -1)
    wide = jnp.concatenate([before, fields, after], axis=2)

    rows = wide.shape[3]
    shape = wide.shape[:3] + (width,)
    count = shape[0] * shape[1] * shape[2] * shape[3]

    def pack(lo, hi):
        part = wide[:, :, :, lo:hi].reshape(-1)
        rates = shifts[:, lo:hi].astype(jnp.float32).reshape(-1)
        return jnp.concatenate([part, rates])

    def unpack(flat):
        part = flat[:count].reshape(shape)
        rates = flat[count:].reshape(shifts.shape[0], width)
        return part, rates.astype(jnp.int32)

    inner, inner_shift = unpack(passed_along(pack(rows - width, rows), "rad", 1, False))
    outer, outer_shift = unpack(passed_along(pack(0, width), "rad", -1, False))
    wide = jnp.concatenate([inner, wide, outer], axis=3)
    wide_shifts = jnp.concatenate([inner_shift, shifts, outer_shift], axis=1)
    return wide, wide_shifts


def rotate_window(window, offsets, out_len):
    take = SMAX - offsets
    nbits = SMAX.bit_length()
    spare = (1 << nbits) - 1 + out_len - window.shape[2]
    if spare > 0:
        pad = jnp.zeros(window.shape[:2] + (spare,) + window.shape[3:], window.dtype)
        window = jnp.concatenate([window, pad], axis=2)
    for bit in range(nbits):
        amount = 1 << bit
        length = window.shape[2] - amount
        chosen = take // amount % 2 == 1
        window = jnp.where(
            chosen[None, None, None, :], window[:, :, amount:], window[:, :, :length]
        )
    return window[:, :, :out_len]


def relay_seat(lane, source, plane, blocks):
    if source // 2 == lane:
        return source
    if 2 * lane + 1 < plane - blocks and 2 * lane < blocks:
        return 2 * lane + 1
    return 2 * lane


def crossing_relays(groups, count, plane, blocks):
    half = plane // 2
    first, second = [], []
    for g in range(groups):
        for block in range(count // plane):
            base = block * plane
            after = (base + plane) % count
            for j in range(1, blocks + 1):
                lane = (3 * g + j + 1) % half
                relay = base + relay_seat(lane, plane - j, plane, blocks)
                first.append((g * count + base + plane - j, g * count + relay))
                second.append((g * count + relay, g * count + after + blocks - j))
    return first, second


def rotation_pieces(head, plane, blocks):
    count = lax.axis_size("azi")
    groups = lax.axis_size("rad")
    if count % plane or count <= plane or plane < 2 * blocks:
        return [passed_along(head, "azi", k) for k in range(1, blocks + 1)]
    near = []
    for k in range(1, blocks + 1):
        pairs = [
            (a, (a + k) % count)
            for a in range(count)
            if a // plane == ((a + k) % count) // plane
        ]
        near.append(lax.ppermute(head, "azi", pairs))
    first, second = crossing_relays(groups, count, plane, blocks)
    relayed = lax.ppermute(head, ("rad", "azi"), first)
    crossed = lax.ppermute(relayed, ("rad", "azi"), second)
    direct = [
        (a, b - (blocks - 1))
        for a, b in second
        if (b % plane) == blocks - 1
    ]
    first_seat = lax.ppermute(relayed, ("rad", "azi"), direct)
    position = lax.axis_index("azi") % plane
    pieces = []
    for k in range(1, blocks + 1):
        if k == blocks:
            far = crossed
        elif k == 1 and blocks > 1:
            far = first_seat
        else:
            t = blocks - k
            pairs = [
                (base + i + t, base + i)
                for base in range(0, count, plane)
                for i in range(blocks - t)
            ]
            far = lax.ppermute(crossed, "azi", pairs)
        pieces.append(jnp.where(position < k, far, near[k - 1]))
    return pieces


def local(fields, shifts):
    cells = fields.shape[2]
    rows = fields.shape[3]
    total_rows = rows * lax.axis_size("rad")
    width = STEPS
    wide, wide_shifts = halo_exchange(fields, shifts, width)
    start_row = lax.axis_index("rad") * rows
    blocks = (SMAX + cells - 1) // cells
    for step in range(STEPS):
        w = width - step
        row_index = start_row - w + jnp.arange(rows + 2 * w, dtype=jnp.int32)
        inside = (row_index >= 0) & (row_index < total_rows)
        wide = jnp.where(inside[None, None, None, :], wide, 0.0)
        inner_rows = row_index[1:-1]
        radius = 1.0 + (inner_rows.astype(jnp.float32) + 0.5) / jnp.float32(total_rows)
        inverse = 1.0 / radius
        updated = update(wide, inverse)
        a = w - 1
        head = updated[:, :, :cells]
        pieces = rotation_pieces(head, PLANE, blocks)
        window = jnp.concatenate(pieces[::-1] + [updated], axis=2)
        window = window[:, :, blocks * cells - SMAX :]
        wide_shifts = wide_shifts[:, 1:-1]
        wide = rotate_window(window, wide_shifts[step], cells + 2 * a)
    return wide


def solution(mesh):
    placed = (P(None, None, "azi", "rad"), P(None, "rad"))
    return jax.shard_map(
        local, mesh=mesh, in_specs=placed, out_specs=P(None, None, "azi", "rad"), check_vma=False
    )
```
